512 devices in a mesh: chan: 16 (over z_hi, x), bl: 32 (over y, z_lo, core).
Axes of the slice: x: 4, y: 8, z: 8 (z_hi: 4, z_lo: 2; z = z_hi * 2 + z_lo), core: 2. Of those that a mesh axis runs over, the one named last changes fastest.
Arguments:
- grid: float32 [256, 128, 256], P('bl'), may hold values from -6 to 6
- tile_list: int32 [16, 2048], P('chan', 'bl'), may hold values from 0 to 255, as said below
- owner_map: int32 [256], replicated, may hold values from 0 to 255, as said below
- offsets: int32 [16, 2048, 2], P('chan', 'bl'), may hold values from 4 to 60
- positions: float32 [16, 2048, 2, 128], P('chan', 'bl'), may hold values from 0 to 64
- observed: float32 [16, 2048, 2, 128], P('chan', 'bl'), may hold values from -6 to 6
- weights: float32 [16, 2048, 128], P('chan', 'bl'), may hold values from 0.1 to 1
Outputs:
- new_grid: float32 [256, 128, 256], P('bl', 'chan')
- residual: float32 [16, 2048, 2, 128], P('chan', 'bl')
The draws below stay inside these ranges and needn't reach their ends.
Inputs may be any that keep to these rules, and one draw needn't show every extreme that they name: A permutation: tile t lies on index owner_map[t] // 8 of bl, at place owner_map[t] % 8 there. `tile_list`: of the 64 blocks held by one device (one channel group, one index of bl), at most 4 name tiles of any one owner; in every channel group some owner receives exactly 4 blocks from every device of that group.
All inputs are finite; a program needn't handle non-finite values.
Results may differ from the reference program's by a relative error of at most 0.008.
Values sent between devices are 32-bit elements; how exact they have to be, the bound alone decides.
No kernel may reach another device: no remote copies, remote signals or barrier semaphores. Data moves between devices by JAX's collectives and lax.ppermute only.
A program may use at most 128 MiB of HBM per device.

```python
import math
import jax
import jax.numpy as jnp
from jax import lax

TILE = 128
VIS = 128
BLK_DEV = 64
TILE_DEV = 8
GROUPS = 16
BLOCKS = 2048
TILES = 256
SPAN = 64


def slot_table(key):
    return jax.random.permutation(jax.random.fold_in(key, 7), TILES).astype(jnp.int32)


def draw_owner_map(key, part):
    return slot_table(key)


def draw_tile_list(key, part):
    slots = slot_table(key)
    tile_of_slot = jnp.argsort(slots, stable=True).astype(jnp.int32)
    owners = BLOCKS // BLK_DEV
    capacity = 2 * (BLK_DEV // owners)
    route_key = jax.random.fold_in(key, 11)

    def one_device(group_id, member_id):
        group_key = jax.random.fold_in(route_key, group_id)
        hot_owner = jax.random.randint(group_key, (), 0, owners)
        device_key = jax.random.fold_in(group_key, member_id + 1000)
        key_list = jax.random.split(device_key, 4)
        order = jax.random.permutation(key_list[0], owners - 1).astype(jnp.int32)
        others = order + (order >= hot_owner).astype(jnp.int32)
        pairs = others[1:].reshape(owners // 2 - 1, 2)
        splits = jax.random.randint(key_list[1], (owners // 2 - 1,), 0, capacity + 1)
        counts = jnp.zeros((owners,), jnp.int32).at[hot_owner].set(capacity)
        counts = counts.at[pairs[:, 0]].set(splits).at[pairs[:, 1]].set(capacity - splits)
        bounds = jnp.cumsum(counts)
        places = jnp.arange(BLK_DEV, dtype=jnp.int32)
        owner_seq = jnp.sum((places[:, None] >= bounds[None, :]).astype(jnp.int32), axis=1)
        owner_seq = jax.random.permutation(key_list[2], owner_seq)
        local_slot = jax.random.randint(key_list[3], (BLK_DEV,), 0, TILE_DEV)
        return tile_of_slot[owner_seq * TILE_DEV + local_slot]

    def one_group(group_id):
        return jax.vmap(lambda member_id: one_device(group_id, member_id))(jnp.arange(owners))
    table = jax.vmap(one_group)(jnp.arange(GROUPS))
    return table.reshape(GROUPS, BLOCKS).astype(jnp.int32)


def place_ends(result, rng, least, top_value):
    place = [jax.random.randint(jax.random.fold_in(rng, axis), (), 0, length) for axis, length in enumerate(result.shape)]
    widest = result.shape.index(max(result.shape))
    next_to = place[:widest] + [(place[widest] + 1) % result.shape[widest]] + place[widest + 1:]
    return result.at[tuple(place)].set(least).at[tuple(next_to)].set(top_value)


def level_of(own_key, extent, cuts, smallest, largest):
    level = 1.0
    for position, parts in cuts:
        heights = jax.random.uniform(jax.random.fold_in(jax.random.fold_in(own_key, 6), position), (parts,), jnp.float32, smallest / len(cuts), largest / len(cuts))
        level = level * jnp.repeat(jnp.exp(heights), extent[position] // parts).reshape((-1,) + (1,) * (len(extent) - 1 - position))
    return level


def centred(rng, shape, deviation, limit, cuts=(), held_as=jnp.bfloat16):
    factor_of = level_of(rng, shape, cuts, -0.22, 0.18) if cuts else 1.0
    drawn = jax.random.normal(rng, shape, jnp.float32) * deviation * factor_of
    return jnp.minimum(jnp.maximum(drawn, -limit), limit).astype(held_as)


def setup_inputs(seed: int = 0) -> dict:
    seeds = jax.random.split(jax.random.key(seed), 8)
    return {
        "grid": centred(seeds[0], (TILES, TILE, 2 * TILE), 1.0, 6.0, ((0, 32),), jnp.float32),
        "tile_list": draw_tile_list(jax.random.fold_in(seeds[7], 71), 0),
        "owner_map": draw_owner_map(jax.random.fold_in(seeds[7], 71), 0),
        "offsets": place_ends(jax.random.randint(seeds[3], (GROUPS, BLOCKS, 2), 4, SPAN - 3), jax.random.fold_in(seeds[3], 1), 4, (SPAN - 3) - 1).astype(jnp.int32),
        "positions": jnp.clip(64.0 * jax.random.uniform(seeds[4], (GROUPS, BLOCKS, 2, VIS), jnp.float32) ** level_of(seeds[4], (GROUPS, BLOCKS, 2, VIS), ((0, 16), (1, 32)), -0.2, 0.2), 0.0, 64.0),
        "observed": centred(seeds[5], (GROUPS, BLOCKS, 2, VIS), 1.0, 6.0, ((0, 16), (1, 32)), jnp.float32),
        "weights": jnp.clip(jnp.exp(math.log(1.0) - 2.3025851 * jax.random.uniform(seeds[6], (GROUPS, BLOCKS, VIS), jnp.float32) ** level_of(seeds[6], (GROUPS, BLOCKS, VIS), ((0, 16), (1, 32)), -0.2, 0.2)), 0.1, 1.0),
    }


kernel_beta = 18.4
half_support = 4.0
step_length = 1.0
ridge_weight = 0.5

def spheroid(offset):
    scaled = offset / half_support
    inside = scaled * scaled < 1.0
    root_term = jnp.sqrt(jnp.maximum(1.0 - scaled * scaled, 0.0))
    return jnp.where(inside, jnp.exp(kernel_beta * (root_term - 1.0)), 0.0)

def reference(grid, tile_list, owner_map, offsets, positions, observed, weights):
    tile_width = grid.shape[1]
    grid_low = lax.optimization_barrier(grid.astype(jnp.bfloat16)).astype(jnp.float32)
    tap_offsets = jnp.arange(8, dtype=jnp.int32)

    def one_group(gradient, block_item):
        tile_ids, shift, fraction, observed_now, weight_now = block_item
        slot_index = owner_map[tile_ids].astype(jnp.int32)
        coords = shift.astype(jnp.float32)[..., None] + fraction
        first_cell = jnp.floor(coords).astype(jnp.int32) - 3
        cell_taps = first_cell[..., None] + tap_offsets
        kernel_taps = spheroid(cell_taps.astype(jnp.float32) - coords[..., None]).astype(jnp.bfloat16)
        kernel_taps = lax.optimization_barrier(kernel_taps).astype(jnp.float32)
        kernel_u = kernel_taps[:, 0]
        kernel_v = kernel_taps[:, 1]
        slot_grid = slot_index[:, None, None, None]
        u_rows = cell_taps[:, 0][:, :, :, None]
        v_cols = cell_taps[:, 1][:, :, None, :]
        patch_real = grid_low[slot_grid, u_rows, v_cols]
        patch_imag = grid_low[slot_grid, u_rows, v_cols + tile_width]
        weight_taps = kernel_u[..., :, None] * kernel_v[..., None, :]
        model_real = lax.optimization_barrier(jnp.sum(weight_taps * patch_real, axis=(2, 3)))
        model_imag = lax.optimization_barrier(jnp.sum(weight_taps * patch_imag, axis=(2, 3)))
        residual_now = weight_now[:, None, :] * (jnp.stack([model_real, model_imag], axis=1) - observed_now)
        spread_real = lax.optimization_barrier((residual_now[:, 0, :, None] * kernel_v).astype(jnp.bfloat16)).astype(jnp.float32)
        spread_imag = lax.optimization_barrier((residual_now[:, 1, :, None] * kernel_v).astype(jnp.bfloat16)).astype(jnp.float32)
        update_real = kernel_u[..., :, None] * spread_real[..., None, :]
        update_imag = kernel_u[..., :, None] * spread_imag[..., None, :]
        gradient = gradient.at[slot_grid, u_rows, v_cols].add(update_real)
        gradient = gradient.at[slot_grid, u_rows, v_cols + tile_width].add(update_imag)
        return (gradient, residual_now)
    start_grad = jnp.zeros(grid.shape, jnp.float32)
    gradient, residual = lax.scan(one_group, start_grad, (tile_list, offsets, positions, observed, weights))
    new_grid = grid - step_length * (gradient + ridge_weight * grid)
    return (new_grid, residual)
```

```python
import functools

import jax
import jax.numpy as jnp
from jax import lax
from jax.experimental import pallas as pl
from jax.experimental.pallas import tpu as pltpu
from jax.sharding import PartitionSpec as P

kernel_beta = 18.4
half_support = 4.0
step_length = 1.0
ridge_weight = 0.5


def spheroid(offset):
    scaled = offset * (1.0 / half_support)
    inside = scaled * scaled < 1.0
    root_term = jnp.sqrt(jnp.maximum(1.0 - scaled * scaled, 0.0))
    return jnp.where(inside, jnp.exp(kernel_beta * (root_term - 1.0)), 0.0)


def _grid_kernel(labels_ref, data_ref, tiles_ref, res_ref, grad_ref):
    slots = data_ref.shape[0]
    width = tiles_ref.shape[2]
    vis = data_ref.shape[2]
    grad_ref[...] = jnp.zeros(grad_ref.shape, grad_ref.dtype)
    cells = lax.broadcasted_iota(jnp.int32, (width, vis), 0).astype(jnp.float32)

    def body(s, carry):
        d = data_ref[s]
        tile = labels_ref[s]
        ku_t = spheroid(cells - d[3:4, :]).astype(jnp.bfloat16)
        kv_t = spheroid(cells - d[4:5, :]).astype(jnp.bfloat16).astype(jnp.float32)
        proj_t = jnp.dot(tiles_ref[tile], ku_t, preferred_element_type=jnp.float32)
        model_re = jnp.sum(proj_t[:width] * kv_t, axis=0, keepdims=True)
        model_im = jnp.sum(proj_t[width:] * kv_t, axis=0, keepdims=True)
        weight = d[2:3, :]
        res_re = weight * (model_re - d[0:1, :])
        res_im = weight * (model_im - d[1:2, :])
        res_ref[s] = jnp.concatenate([res_re, res_im], axis=0)
        spread_t = jnp.concatenate([res_re * kv_t, res_im * kv_t], axis=0).astype(jnp.bfloat16)
        contrib = lax.dot_general(
            ku_t, spread_t, (((1,), (1,)), ((), ())), preferred_element_type=jnp.float32
        )
        grad_ref[tile] += contrib
        return carry

    lax.fori_loop(0, slots, body, 0)


def _grid_call(labels, data, tiles_t):
    slots, _, vis = data.shape
    tile_count, wide, width = tiles_t.shape
    vmem = pltpu.MemorySpace.VMEM
    return pl.pallas_call(
        _grid_kernel,
        out_shape=(
            jax.ShapeDtypeStruct((slots, 2, vis), jnp.float32),
            jax.ShapeDtypeStruct((tile_count, width, wide), jnp.float32),
        ),
        in_specs=[
            pl.BlockSpec(memory_space=pltpu.MemorySpace.SMEM),
            pl.BlockSpec(memory_space=vmem),
            pl.BlockSpec(memory_space=vmem),
        ],
        out_specs=(pl.BlockSpec(memory_space=vmem), pl.BlockSpec(memory_space=vmem)),
    )(labels, data, tiles_t)


def shards(grid, tile_list, owner_map, offsets, positions, observed, weights):
    owners = lax.axis_size("bl")
    chan = lax.axis_size("chan")
    tile_dev = grid.shape[0]
    tile_width = grid.shape[1]
    block_count = tile_list.shape[1]
    capacity = 2 * block_count // owners
    slots_all = owners * capacity
    tile_ids = tile_list[0]
    slot_index = jnp.take(owner_map, tile_ids, axis=0)
    owner_index = slot_index // tile_dev
    local_slot = slot_index % tile_dev
    owner_onehot = (owner_index[:, None] == jnp.arange(owners, dtype=jnp.int32)[None, :]).astype(
        jnp.int32
    )
    earlier_count = jnp.cumsum(owner_onehot, axis=0) - owner_onehot
    place_rank = jnp.sum(owner_onehot * earlier_count, axis=1)
    send_slot = owner_index * capacity + place_rank
    coords = offsets[0].astype(jnp.float32)[..., None] + positions[0]
    vis = coords.shape[-1]
    label_row = jnp.broadcast_to(local_slot.astype(jnp.float32)[:, None, None], (block_count, 1, vis))
    payload = jnp.concatenate([observed[0], weights[0][:, None, :], coords, label_row], axis=1)
    match = send_slot[None, :] == jnp.arange(slots_all, dtype=jnp.int32)[:, None]
    source = jnp.sum(jnp.where(match, jnp.arange(block_count, dtype=jnp.int32)[None, :], 0), axis=1)
    filled = jnp.any(match, axis=1)
    outgoing = jnp.where(filled[:, None, None], jnp.take(payload, source, axis=0), 0.0)
    incoming = lax.all_to_all(outgoing, "bl", split_axis=0, concat_axis=0, tiled=True)
    labels = incoming[:, 5, 0].astype(jnp.int32)
    tiles_t = jnp.swapaxes(grid.astype(jnp.bfloat16), 1, 2)
    residual_all, gradient = _grid_call(labels, incoming, tiles_t)
    share_rows = tile_width // chan
    parts = gradient.reshape(tile_dev, chan, share_rows, gradient.shape[-1])
    parts = lax.all_to_all(parts, "chan", split_axis=1, concat_axis=1, tiled=True)
    grad_share = jnp.sum(parts, axis=1)
    returned = lax.all_to_all(residual_all, "bl", split_axis=0, concat_axis=0, tiled=True)
    my_residual = jnp.take(returned, send_slot, axis=0)[None]
    share_start = lax.axis_index("chan") * share_rows
    own_rows = lax.dynamic_slice_in_dim(grid, share_start, share_rows, 1)
    new_grid = own_rows - step_length * (grad_share + ridge_weight * own_rows)
    return (new_grid, my_residual)


def solution(mesh):
    in_specs = (
        P("bl", None, None),
        P("chan", "bl"),
        P(),
        P("chan", "bl", None),
        P("chan", "bl", None, None),
        P("chan", "bl", None, None),
        P("chan", "bl", None),
    )
    out_specs = (P("bl", "chan", None), P("chan", "bl", None, None))
    return jax.shard_map(shards, mesh=mesh, in_specs=in_specs, out_specs=out_specs, check_vma=False)
```

```python
import functools

import jax
import jax.numpy as jnp
from jax import lax
from jax.experimental import pallas as pl
from jax.experimental.pallas import tpu as pltpu
from jax.sharding import PartitionSpec as P

kernel_beta = 18.4
half_support = 4.0
step_length = 1.0
ridge_weight = 0.5


def spheroid(offset):
    scaled = offset * (1.0 / half_support)
    inside = scaled * scaled < 1.0
    root_term = jnp.sqrt(jnp.maximum(1.0 - scaled * scaled, 0.0))
    return jnp.where(inside, jnp.exp(kernel_beta * (root_term - 1.0)), 0.0)


def _grid_kernel(labels_ref, data_ref, tiles_ref, res_ref, grad_ref):
    slots = data_ref.shape[0]
    width = tiles_ref.shape[2]
    vis = data_ref.shape[2]
    grad_ref[...] = jnp.zeros(grad_ref.shape, grad_ref.dtype)
    cells = lax.broadcasted_iota(jnp.int32, (width, vis), 0).astype(jnp.float32)

    def body(s, carry):
        d = data_ref[s]
        tile = labels_ref[s]
        ku_t = spheroid(cells - d[3:4, :]).astype(jnp.bfloat16)
        kv_t = spheroid(cells - d[4:5, :]).astype(jnp.bfloat16).astype(jnp.float32)
        proj_t = jnp.dot(tiles_ref[tile], ku_t, preferred_element_type=jnp.float32)
        model_re = jnp.sum(proj_t[:width] * kv_t, axis=0, keepdims=True)
        model_im = jnp.sum(proj_t[width:] * kv_t, axis=0, keepdims=True)
        weight = d[2:3, :]
        res_re = weight * (model_re - d[0:1, :])
        res_im = weight * (model_im - d[1:2, :])
        res_ref[s] = jnp.concatenate([res_re, res_im], axis=0)
        spread_t = jnp.concatenate([res_re * kv_t, res_im * kv_t], axis=0).astype(jnp.bfloat16)
        contrib = lax.dot_general(
            ku_t, spread_t, (((1,), (1,)), ((), ())), preferred_element_type=jnp.float32
        )
        grad_ref[tile] += contrib
        return carry

    lax.fori_loop(0, slots, body, 0, unroll=16)


def _grid_call(labels, data, tiles_t):
    slots, _, vis = data.shape
    tile_count, wide, width = tiles_t.shape
    vmem = pltpu.MemorySpace.VMEM
    return pl.pallas_call(
        _grid_kernel,
        out_shape=(
            jax.ShapeDtypeStruct((slots, 2, vis), jnp.float32),
            jax.ShapeDtypeStruct((tile_count, width, wide), jnp.float32),
        ),
        in_specs=[
            pl.BlockSpec(memory_space=pltpu.MemorySpace.SMEM),
            pl.BlockSpec(memory_space=vmem),
            pl.BlockSpec(memory_space=vmem),
        ],
        out_specs=(pl.BlockSpec(memory_space=vmem), pl.BlockSpec(memory_space=vmem)),
    )(labels, data, tiles_t)


def shards(grid, tile_list, owner_map, offsets, positions, observed, weights):
    owners = lax.axis_size("bl")
    chan = lax.axis_size("chan")
    tile_dev = grid.shape[0]
    tile_width = grid.shape[1]
    block_count = tile_list.shape[1]
    capacity = 2 * block_count // owners
    slots_all = owners * capacity
    tile_ids = tile_list[0]
    slot_index = jnp.take(owner_map, tile_ids, axis=0)
    owner_index = slot_index // tile_dev
    local_slot = slot_index % tile_dev
    owner_onehot = (owner_index[:, None] == jnp.arange(owners, dtype=jnp.int32)[None, :]).astype(
        jnp.int32
    )
    earlier_count = jnp.cumsum(owner_onehot, axis=0) - owner_onehot
    place_rank = jnp.sum(owner_onehot * earlier_count, axis=1)
    send_slot = owner_index * capacity + place_rank
    coords = offsets[0].astype(jnp.float32)[..., None] + positions[0]
    payload = jnp.concatenate([observed[0], weights[0][:, None, :], coords], axis=1)
    match = send_slot[None, :] == jnp.arange(slots_all, dtype=jnp.int32)[:, None]
    source = jnp.sum(jnp.where(match, jnp.arange(block_count, dtype=jnp.int32)[None, :], 0), axis=1)
    filled = jnp.any(match, axis=1)
    outgoing = jnp.where(filled[:, None, None], jnp.take(payload, source, axis=0), 0.0)
    incoming = lax.all_to_all(outgoing, "bl", split_axis=0, concat_axis=0, tiled=True)
    tiles_all = lax.all_gather(tile_ids, "bl")
    slot_all = jnp.take(owner_map, tiles_all, axis=0)
    mine = (slot_all // tile_dev == lax.axis_index("bl")).astype(jnp.int32)
    rank_all = jnp.cumsum(mine, axis=1) - 1
    pick = (mine[:, :, None] == 1) & (
        rank_all[:, :, None] == jnp.arange(capacity, dtype=jnp.int32)[None, None, :]
    )
    labels = jnp.sum(jnp.where(pick, (slot_all % tile_dev)[:, :, None], 0), axis=1).reshape(slots_all)
    tiles_t = jnp.swapaxes(grid.astype(jnp.bfloat16), 1, 2)
    residual_all, gradient = _grid_call(labels, incoming, tiles_t)
    share_rows = tile_width // chan
    parts = gradient.reshape(tile_dev, chan, share_rows, gradient.shape[-1])
    parts = lax.all_to_all(parts, "chan", split_axis=1, concat_axis=1, tiled=True)
    grad_share = jnp.sum(parts, axis=1)
    returned = lax.all_to_all(residual_all, "bl", split_axis=0, concat_axis=0, tiled=True)
    my_residual = jnp.take(returned, send_slot, axis=0)[None]
    share_start = lax.axis_index("chan") * share_rows
    own_rows = lax.dynamic_slice_in_dim(grid, share_start, share_rows, 1)
    new_grid = own_rows - step_length * (grad_share + ridge_weight * own_rows)
    return (new_grid, my_residual)


def solution(mesh):
    in_specs = (
        P("bl", None, None),
        P("chan", "bl"),
        P(),
        P("chan", "bl", None),
        P("chan", "bl", None, None),
        P("chan", "bl", None, None),
        P("chan", "bl", None),
    )
    out_specs = (P("bl", "chan", None), P("chan", "bl", None, None))
    return jax.shard_map(shards, mesh=mesh, in_specs=in_specs, out_specs=out_specs, check_vma=False)
```

```python
import functools

import jax
import jax.numpy as jnp
from jax import lax
from jax.experimental import pallas as pl
from jax.experimental.pallas import tpu as pltpu
from jax.sharding import PartitionSpec as P

kernel_beta = 18.4
half_support = 4.0
step_length = 1.0
ridge_weight = 0.5


def spheroid(offset):
    scaled = offset * (1.0 / half_support)
    inside = scaled * scaled < 1.0
    root_term = jnp.sqrt(jnp.maximum(1.0 - scaled * scaled, 0.0))
    return jnp.where(inside, jnp.exp(kernel_beta * (root_term - 1.0)), 0.0)


def _grid_kernel(labels_ref, data_ref, tiles_ref, res_ref, grad_ref):
    slots = data_ref.shape[0]
    chunks, _, rows, _ = grad_ref.shape
    width = tiles_ref.shape[2]
    vis = data_ref.shape[2]
    grad_ref[...] = jnp.zeros(grad_ref.shape, grad_ref.dtype)
    cells = lax.broadcasted_iota(jnp.int32, (width, vis), 0).astype(jnp.float32)

    def body(s, carry):
        d = data_ref[s]
        tile = labels_ref[s]
        ku_t = spheroid(cells - d[3:4, :]).astype(jnp.bfloat16)
        kv_t = spheroid(cells - d[4:5, :]).astype(jnp.bfloat16).astype(jnp.float32)
        proj_t = jnp.dot(tiles_ref[tile], ku_t, preferred_element_type=jnp.float32)
        model_re = jnp.sum(proj_t[:width] * kv_t, axis=0, keepdims=True)
        model_im = jnp.sum(proj_t[width:] * kv_t, axis=0, keepdims=True)
        weight = d[2:3, :]
        res_re = weight * (model_re - d[0:1, :])
        res_im = weight * (model_im - d[1:2, :])
        res_ref[s] = jnp.concatenate([res_re, res_im], axis=0)
        spread_t = jnp.concatenate([res_re * kv_t, res_im * kv_t], axis=0).astype(jnp.bfloat16)
        contrib = lax.dot_general(
            ku_t, spread_t, (((1,), (1,)), ((), ())), preferred_element_type=jnp.float32
        )
        grad_ref[:, pl.ds(tile, 1)] += contrib.reshape(chunks, 1, rows, 2 * width)
        return carry

    lax.fori_loop(0, slots, body, 0, unroll=16)


def _grid_call(labels, data, tiles_t, chunks):
    slots, _, vis = data.shape
    tile_count, wide, width = tiles_t.shape
    vmem = pltpu.MemorySpace.VMEM
    return pl.pallas_call(
        _grid_kernel,
        out_shape=(
            jax.ShapeDtypeStruct((slots, 2, vis), jnp.float32),
            jax.ShapeDtypeStruct((chunks, tile_count, width // chunks, wide), jnp.float32),
        ),
        in_specs=[
            pl.BlockSpec(memory_space=pltpu.MemorySpace.SMEM),
            pl.BlockSpec(memory_space=vmem),
            pl.BlockSpec(memory_space=vmem),
        ],
        out_specs=(pl.BlockSpec(memory_space=vmem), pl.BlockSpec(memory_space=vmem)),
    )(labels, data, tiles_t)


def shards(grid, tile_list, owner_map, offsets, positions, observed, weights):
    owners = lax.axis_size("bl")
    chan = lax.axis_size("chan")
    tile_dev = grid.shape[0]
    tile_width = grid.shape[1]
    block_count = tile_list.shape[1]
    capacity = 2 * block_count // owners
    slots_all = owners * capacity
    tile_ids = tile_list[0]
    slot_index = jnp.take(owner_map, tile_ids, axis=0)
    owner_index = slot_index // tile_dev
    local_slot = slot_index % tile_dev
    owner_onehot = (owner_index[:, None] == jnp.arange(owners, dtype=jnp.int32)[None, :]).astype(
        jnp.int32
    )
    earlier_count = jnp.cumsum(owner_onehot, axis=0) - owner_onehot
    place_rank = jnp.sum(owner_onehot * earlier_count, axis=1)
    send_slot = owner_index * capacity + place_rank
    coords = offsets[0].astype(jnp.float32)[..., None] + positions[0]
    vis = coords.shape[-1]
    label_row = jnp.broadcast_to(local_slot.astype(jnp.float32)[:, None, None], (block_count, 1, vis))
    payload = jnp.concatenate([observed[0], weights[0][:, None, :], coords, label_row], axis=1)
    match = send_slot[None, :] == jnp.arange(slots_all, dtype=jnp.int32)[:, None]
    source = jnp.sum(jnp.where(match, jnp.arange(block_count, dtype=jnp.int32)[None, :], 0), axis=1)
    filled = jnp.any(match, axis=1)
    outgoing = jnp.where(filled[:, None, None], jnp.take(payload, source, axis=0), 0.0)
    incoming = lax.all_to_all(outgoing, "bl", split_axis=0, concat_axis=0, tiled=True)
    labels = jnp.max(incoming[:, 5, :], axis=1).astype(jnp.int32)
    tiles_t = jnp.swapaxes(grid.astype(jnp.bfloat16), 1, 2)
    residual_all, gradient = _grid_call(labels, incoming, tiles_t, chan)
    share_rows = tile_width // chan
    parts = lax.all_to_all(gradient, "chan", split_axis=0, concat_axis=0, tiled=True)
    grad_share = jnp.sum(parts, axis=0)
    returned = lax.all_to_all(residual_all, "bl", split_axis=0, concat_axis=0, tiled=True)
    my_residual = jnp.take(returned, send_slot, axis=0)[None]
    share_start = lax.axis_index("chan") * share_rows
    own_rows = lax.dynamic_slice_in_dim(grid, share_start, share_rows, 1)
    new_grid = own_rows - step_length * (grad_share + ridge_weight * own_rows)
    return (new_grid, my_residual)


def solution(mesh):
    in_specs = (
        P("bl", None, None),
        P("chan", "bl"),
        P(),
        P("chan", "bl", None),
        P("chan", "bl", None, None),
        P("chan", "bl", None, None),
        P("chan", "bl", None),
    )
    out_specs = (P("bl", "chan", None), P("chan", "bl", None, None))
    return jax.shard_map(shards, mesh=mesh, in_specs=in_specs, out_specs=out_specs, check_vma=False)
```

```python
import functools

import jax
import jax.numpy as jnp
from jax import lax
from jax.experimental import pallas as pl
from jax.experimental.pallas import tpu as pltpu
from jax.sharding import PartitionSpec as P

kernel_beta = 18.4
half_support = 4.0
step_length = 1.0
ridge_weight = 0.5


def spheroid(offset):
    scaled = offset * (1.0 / half_support)
    inside = scaled * scaled < 1.0
    root_term = jnp.sqrt(jnp.maximum(1.0 - scaled * scaled, 0.0))
    return jnp.where(inside, jnp.exp(kernel_beta * (root_term - 1.0)), 0.0)


def _grid_kernel(labels_ref, data_ref, tiles_ref, res_ref, grad_ref):
    slots = data_ref.shape[0]
    chunks, _, rows, _ = grad_ref.shape
    width = tiles_ref.shape[2]
    vis = data_ref.shape[2]
    grad_ref[...] = jnp.zeros(grad_ref.shape, grad_ref.dtype)
    cells = lax.broadcasted_iota(jnp.int32, (width, vis), 0).astype(jnp.float32)

    def body(s, carry):
        d = data_ref[s]
        tile = labels_ref[s]
        ku_t = spheroid(cells - d[3:4, :]).astype(jnp.bfloat16)
        kv_t = spheroid(cells - d[4:5, :]).astype(jnp.bfloat16).astype(jnp.float32)
        proj_t = jnp.dot(tiles_ref[tile], ku_t, preferred_element_type=jnp.float32)
        model_re = jnp.sum(proj_t[:width] * kv_t, axis=0, keepdims=True)
        model_im = jnp.sum(proj_t[width:] * kv_t, axis=0, keepdims=True)
        weight = d[2:3, :]
        res_re = weight * (model_re - d[0:1, :])
        res_im = weight * (model_im - d[1:2, :])
        res_ref[s] = jnp.concatenate([res_re, res_im], axis=0)
        spread_t = jnp.concatenate([res_re * kv_t, res_im * kv_t], axis=0).astype(jnp.bfloat16)
        contrib = lax.dot_general(
            ku_t, spread_t, (((1,), (1,)), ((), ())), preferred_element_type=jnp.float32
        )
        grad_ref[:, pl.ds(tile, 1)] += contrib.reshape(chunks, 1, rows, 2 * width)
        return carry

    lax.fori_loop(0, slots, body, 0, unroll=16)


def _grid_call(labels, data, tiles_t, chunks):
    slots, _, vis = data.shape
    tile_count, wide, width = tiles_t.shape
    vmem = pltpu.MemorySpace.VMEM
    return pl.pallas_call(
        _grid_kernel,
        out_shape=(
            jax.ShapeDtypeStruct((slots, 2, vis), jnp.float32),
            jax.ShapeDtypeStruct((chunks, tile_count, width // chunks, wide), jnp.float32),
        ),
        in_specs=[
            pl.BlockSpec(memory_space=pltpu.MemorySpace.SMEM),
            pl.BlockSpec(memory_space=vmem),
            pl.BlockSpec(memory_space=vmem),
        ],
        out_specs=(pl.BlockSpec(memory_space=vmem), pl.BlockSpec(memory_space=vmem)),
    )(labels, data, tiles_t)


def shards(grid, tile_list, owner_map, offsets, positions, observed, weights):
    owners = lax.axis_size("bl")
    chan = lax.axis_size("chan")
    tile_dev = grid.shape[0]
    tile_width = grid.shape[1]
    block_count = tile_list.shape[1]
    capacity = 2 * block_count // owners
    slots_all = owners * capacity
    tile_ids = tile_list[0]
    slot_index = jnp.take(owner_map, tile_ids, axis=0)
    owner_index = slot_index // tile_dev
    local_slot = slot_index % tile_dev
    owner_onehot = (owner_index[:, None] == jnp.arange(owners, dtype=jnp.int32)[None, :]).astype(
        jnp.int32
    )
    earlier_count = jnp.cumsum(owner_onehot, axis=0) - owner_onehot
    place_rank = jnp.sum(owner_onehot * earlier_count, axis=1)
    send_slot = owner_index * capacity + place_rank
    coords = offsets[0].astype(jnp.float32)[..., None] + positions[0]
    vis = coords.shape[-1]
    label_row = jnp.broadcast_to(local_slot.astype(jnp.float32)[:, None, None], (block_count, 1, vis))
    payload = jnp.concatenate([observed[0], weights[0][:, None, :], coords, label_row], axis=1)
    match = send_slot[None, :] == jnp.arange(slots_all, dtype=jnp.int32)[:, None]
    source = jnp.sum(jnp.where(match, jnp.arange(block_count, dtype=jnp.int32)[None, :], 0), axis=1)
    filled = jnp.any(match, axis=1)
    outgoing = jnp.where(filled[:, None, None], jnp.take(payload, source, axis=0), 0.0)
    incoming = lax.all_to_all(outgoing, "bl", split_axis=0, concat_axis=0, tiled=True)
    labels = jnp.max(incoming[:, 5, :], axis=1).astype(jnp.int32)
    tiles_t = jnp.swapaxes(grid.astype(jnp.bfloat16), 1, 2)
    residual_all, gradient = _grid_call(labels, incoming, tiles_t, chan)
    share_rows = tile_width // chan
    sc_tiles = tile_dev // 4
    sc_share = lax.psum_scatter(gradient[:, :sc_tiles], "chan", scatter_dimension=0, tiled=True)
    parts = lax.all_to_all(gradient[:, sc_tiles:], "chan", split_axis=0, concat_axis=0, tiled=True)
    grad_share = jnp.concatenate([sc_share[0], jnp.sum(parts, axis=0)], axis=0)
    returned = lax.all_to_all(residual_all, "bl", split_axis=0, concat_axis=0, tiled=True)
    my_residual = jnp.take(returned, send_slot, axis=0)[None]
    share_start = lax.axis_index("chan") * share_rows
    own_rows = lax.dynamic_slice_in_dim(grid, share_start, share_rows, 1)
    new_grid = own_rows - step_length * (grad_share + ridge_weight * own_rows)
    return (new_grid, my_residual)


def solution(mesh):
    in_specs = (
        P("bl", None, None),
        P("chan", "bl"),
        P(),
        P("chan", "bl", None),
        P("chan", "bl", None, None),
        P("chan", "bl", None, None),
        P("chan", "bl", None),
    )
    out_specs = (P("bl", "chan", None), P("chan", "bl", None, None))
    return jax.shard_map(shards, mesh=mesh, in_specs=in_specs, out_specs=out_specs, check_vma=False)
```

```python
import functools

import jax
import jax.numpy as jnp
from jax import lax
from jax.experimental import pallas as pl
from jax.experimental.pallas import tpu as pltpu
from jax.sharding import PartitionSpec as P

kernel_beta = 18.4
half_support = 4.0
step_length = 1.0
ridge_weight = 0.5


def spheroid(offset):
    scaled = offset * (1.0 / half_support)
    inside = scaled * scaled < 1.0
    root_term = jnp.sqrt(jnp.maximum(1.0 - scaled * scaled, 0.0))
    return jnp.where(inside, jnp.exp(kernel_beta * (root_term - 1.0)), 0.0)


def _kernels(data, width, cells):
    ku_t = spheroid(cells - data[3:4, :]).astype(jnp.bfloat16)
    kv_t = spheroid(cells - data[4:5, :]).astype(jnp.bfloat16).astype(jnp.float32)
    return ku_t, kv_t


def _degrid_kernel(labels_ref, data_ref, tiles_ref, res_ref):
    slots = data_ref.shape[0]
    width = tiles_ref.shape[2]
    vis = data_ref.shape[2]
    cells = lax.broadcasted_iota(jnp.int32, (width, vis), 0).astype(jnp.float32)

    def body(s, carry):
        d = data_ref[s]
        ku_t, kv_t = _kernels(d, width, cells)
        proj_t = jnp.dot(tiles_ref[labels_ref[s]], ku_t, preferred_element_type=jnp.float32)
        model_re = jnp.sum(proj_t[:width] * kv_t, axis=0, keepdims=True)
        model_im = jnp.sum(proj_t[width:] * kv_t, axis=0, keepdims=True)
        weight = d[2:3, :]
        res_re = weight * (model_re - d[0:1, :])
        res_im = weight * (model_im - d[1:2, :])
        res_ref[s] = jnp.concatenate([res_re, res_im], axis=0)
        return carry

    lax.fori_loop(0, slots, body, 0, unroll=16)


def _spread_kernel(labels_ref, data_ref, res_ref, grad_ref):
    slots = data_ref.shape[0]
    chunks, _, rows, wide = grad_ref.shape
    width = wide // 2
    vis = data_ref.shape[2]
    grad_ref[...] = jnp.zeros(grad_ref.shape, grad_ref.dtype)
    cells = lax.broadcasted_iota(jnp.int32, (width, vis), 0).astype(jnp.float32)

    def body(s, carry):
        d = data_ref[s]
        tile = labels_ref[s]
        ku_t, kv_t = _kernels(d, width, cells)
        r = res_ref[s]
        spread_t = jnp.concatenate([r[0:1] * kv_t, r[1:2] * kv_t], axis=0).astype(jnp.bfloat16)
        contrib = lax.dot_general(
            ku_t, spread_t, (((1,), (1,)), ((), ())), preferred_element_type=jnp.float32
        )
        grad_ref[:, pl.ds(tile, 1)] += contrib.reshape(chunks, 1, rows, wide)
        return carry

    lax.fori_loop(0, slots, body, 0, unroll=16)


def _degrid_call(labels, data, tiles_t):
    slots, _, vis = data.shape
    vmem = pltpu.MemorySpace.VMEM
    return pl.pallas_call(
        _degrid_kernel,
        out_shape=jax.ShapeDtypeStruct((slots, 2, vis), jnp.float32),
        in_specs=[
            pl.BlockSpec(memory_space=pltpu.MemorySpace.SMEM),
            pl.BlockSpec(memory_space=vmem),
            pl.BlockSpec(memory_space=vmem),
        ],
        out_specs=pl.BlockSpec(memory_space=vmem),
    )(labels, data, tiles_t)


def _spread_call(labels, data, residual, tile_count, width, chunks):
    vmem = pltpu.MemorySpace.VMEM
    return pl.pallas_call(
        _spread_kernel,
        out_shape=jax.ShapeDtypeStruct((chunks, tile_count, width // chunks, 2 * width), jnp.float32),
        in_specs=[
            pl.BlockSpec(memory_space=pltpu.MemorySpace.SMEM),
            pl.BlockSpec(memory_space=vmem),
            pl.BlockSpec(memory_space=vmem),
        ],
        out_specs=pl.BlockSpec(memory_space=vmem),
    )(labels, data, residual)


def shards(grid, tile_list, owner_map, offsets, positions, observed, weights):
    owners = lax.axis_size("bl")
    chan = lax.axis_size("chan")
    tile_dev = grid.shape[0]
    tile_width = grid.shape[1]
    block_count = tile_list.shape[1]
    capacity = 2 * block_count // owners
    slots_all = owners * capacity
    tile_ids = tile_list[0]
    slot_index = jnp.take(owner_map, tile_ids, axis=0)
    owner_index = slot_index // tile_dev
    local_slot = slot_index % tile_dev
    owner_onehot = (owner_index[:, None] == jnp.arange(owners, dtype=jnp.int32)[None, :]).astype(
        jnp.int32
    )
    earlier_count = jnp.cumsum(owner_onehot, axis=0) - owner_onehot
    place_rank = jnp.sum(owner_onehot * earlier_count, axis=1)
    send_slot = owner_index * capacity + place_rank
    coords = offsets[0].astype(jnp.float32)[..., None] + positions[0]
    vis = coords.shape[-1]
    label_row = jnp.broadcast_to(local_slot.astype(jnp.float32)[:, None, None], (block_count, 1, vis))
    payload = jnp.concatenate([observed[0], weights[0][:, None, :], coords, label_row], axis=1)
    match = send_slot[None, :] == jnp.arange(slots_all, dtype=jnp.int32)[:, None]
    source = jnp.sum(jnp.where(match, jnp.arange(block_count, dtype=jnp.int32)[None, :], 0), axis=1)
    filled = jnp.any(match, axis=1)
    outgoing = jnp.where(filled[:, None, None], jnp.take(payload, source, axis=0), 0.0)
    incoming = lax.all_to_all(outgoing, "bl", split_axis=0, concat_axis=0, tiled=True)
    labels = jnp.max(incoming[:, 5, :], axis=1).astype(jnp.int32)
    tiles_t = jnp.swapaxes(grid.astype(jnp.bfloat16), 1, 2)
    residual_all = _degrid_call(labels, incoming, tiles_t)
    returned = lax.all_to_all(residual_all, "bl", split_axis=0, concat_axis=0, tiled=True)
    gradient = _spread_call(labels, incoming, residual_all, tile_dev, tile_width, chan)
    share_rows = tile_width // chan
    parts = lax.all_to_all(gradient, "chan", split_axis=0, concat_axis=0, tiled=True)
    grad_share = jnp.sum(parts, axis=0)
    my_residual = jnp.take(returned, send_slot, axis=0)[None]
    share_start = lax.axis_index("chan") * share_rows
    own_rows = lax.dynamic_slice_in_dim(grid, share_start, share_rows, 1)
    new_grid = own_rows - step_length * (grad_share + ridge_weight * own_rows)
    return (new_grid, my_residual)


def solution(mesh):
    in_specs = (
        P("bl", None, None),
        P("chan", "bl"),
        P(),
        P("chan", "bl", None),
        P("chan", "bl", None, None),
        P("chan", "bl", None, None),
        P("chan", "bl", None),
    )
    out_specs = (P("bl", "chan", None), P("chan", "bl", None, None))
    return jax.shard_map(shards, mesh=mesh, in_specs=in_specs, out_specs=out_specs, check_vma=False)
```

```python
import functools

import jax
import jax.numpy as jnp
from jax import lax
from jax.experimental import pallas as pl
from jax.experimental.pallas import tpu as pltpu
from jax.sharding import PartitionSpec as P

kernel_beta = 18.4
half_support = 4.0
step_length = 1.0
ridge_weight = 0.5


def spheroid(offset):
    scaled = offset * (1.0 / half_support)
    inside = scaled * scaled < 1.0
    root_term = jnp.sqrt(jnp.maximum(1.0 - scaled * scaled, 0.0))
    return jnp.where(inside, jnp.exp(kernel_beta * (root_term - 1.0)), 0.0)


def _spheroid_scaled(scaled):
    inside = scaled * scaled < 1.0
    rest = 1.0 - scaled * scaled
    root_term = rest * lax.rsqrt(rest)
    return jnp.where(inside, jnp.exp(kernel_beta * (root_term - 1.0)), 0.0)


def _grid_kernel(labels_ref, data_ref, tiles_ref, res_ref, grad_ref):
    slots = data_ref.shape[0]
    chunks, _, rows, _ = grad_ref.shape
    width = tiles_ref.shape[2]
    vis = data_ref.shape[2]
    grad_ref[...] = jnp.zeros(grad_ref.shape, grad_ref.dtype)
    cells = lax.broadcasted_iota(jnp.int32, (width, vis), 0).astype(jnp.float32) * (1.0 / half_support)

    def body(s, carry):
        d = data_ref[s]
        tile = labels_ref[s]
        quarter = d[3:5, :] * (1.0 / half_support)
        ku_t = _spheroid_scaled(cells - quarter[0:1]).astype(jnp.bfloat16)
        kv_t = _spheroid_scaled(cells - quarter[1:2]).astype(jnp.bfloat16).astype(jnp.float32)
        proj_t = jnp.dot(tiles_ref[tile], ku_t, preferred_element_type=jnp.float32)
        model_re = jnp.sum(proj_t[:width] * kv_t, axis=0, keepdims=True)
        model_im = jnp.sum(proj_t[width:] * kv_t, axis=0, keepdims=True)
        weight = d[2:3, :]
        res_re = weight * (model_re - d[0:1, :])
        res_im = weight * (model_im - d[1:2, :])
        res_ref[s] = jnp.concatenate([res_re, res_im], axis=0)
        spread_t = jnp.concatenate([res_re * kv_t, res_im * kv_t], axis=0).astype(jnp.bfloat16)
        contrib = lax.dot_general(
            ku_t, spread_t, (((1,), (1,)), ((), ())), preferred_element_type=jnp.float32
        )
        grad_ref[:, pl.ds(tile, 1)] += contrib.reshape(chunks, 1, rows, 2 * width)
        return carry

    lax.fori_loop(0, slots, body, 0, unroll=16)


def _grid_call(labels, data, tiles_t, chunks):
    slots, _, vis = data.shape
    tile_count, wide, width = tiles_t.shape
    vmem = pltpu.MemorySpace.VMEM
    return pl.pallas_call(
        _grid_kernel,
        out_shape=(
            jax.ShapeDtypeStruct((slots, 2, vis), jnp.float32),
            jax.ShapeDtypeStruct((chunks, tile_count, width // chunks, wide), jnp.float32),
        ),
        in_specs=[
            pl.BlockSpec(memory_space=pltpu.MemorySpace.SMEM),
            pl.BlockSpec(memory_space=vmem),
            pl.BlockSpec(memory_space=vmem),
        ],
        out_specs=(pl.BlockSpec(memory_space=vmem), pl.BlockSpec(memory_space=vmem)),
    )(labels, data, tiles_t)


def shards(grid, tile_list, owner_map, offsets, positions, observed, weights):
    owners = lax.axis_size("bl")
    chan = lax.axis_size("chan")
    tile_dev = grid.shape[0]
    tile_width = grid.shape[1]
    block_count = tile_list.shape[1]
    capacity = 2 * block_count // owners
    slots_all = owners * capacity
    tile_ids = tile_list[0]
    slot_index = jnp.take(owner_map, tile_ids, axis=0)
    owner_index = slot_index // tile_dev
    local_slot = slot_index % tile_dev
    owner_onehot = (owner_index[:, None] == jnp.arange(owners, dtype=jnp.int32)[None, :]).astype(
        jnp.int32
    )
    earlier_count = jnp.cumsum(owner_onehot, axis=0) - owner_onehot
    place_rank = jnp.sum(owner_onehot * earlier_count, axis=1)
    send_slot = owner_index * capacity + place_rank
    coords = offsets[0].astype(jnp.float32)[..., None] + positions[0]
    vis = coords.shape[-1]
    label_row = jnp.broadcast_to(local_slot.astype(jnp.float32)[:, None, None], (block_count, 1, vis))
    payload = jnp.concatenate([observed[0], weights[0][:, None, :], coords, label_row], axis=1)
    match = send_slot[None, :] == jnp.arange(slots_all, dtype=jnp.int32)[:, None]
    source = jnp.sum(jnp.where(match, jnp.arange(block_count, dtype=jnp.int32)[None, :], 0), axis=1)
    filled = jnp.any(match, axis=1)
    outgoing = jnp.where(filled[:, None, None], jnp.take(payload, source, axis=0), 0.0)
    incoming = lax.all_to_all(outgoing, "bl", split_axis=0, concat_axis=0, tiled=True)
    labels = jnp.max(incoming[:, 5, :], axis=1).astype(jnp.int32)
    tiles_t = jnp.swapaxes(grid.astype(jnp.bfloat16), 1, 2)
    residual_all, gradient = _grid_call(labels, incoming, tiles_t, chan)
    share_rows = tile_width // chan
    parts = lax.all_to_all(gradient, "chan", split_axis=0, concat_axis=0, tiled=True)
    grad_share = jnp.sum(parts, axis=0)
    returned = lax.all_to_all(residual_all, "bl", split_axis=0, concat_axis=0, tiled=True)
    my_residual = jnp.take(returned, send_slot, axis=0)[None]
    share_start = lax.axis_index("chan") * share_rows
    own_rows = lax.dynamic_slice_in_dim(grid, share_start, share_rows, 1)
    new_grid = own_rows - step_length * (grad_share + ridge_weight * own_rows)
    return (new_grid, my_residual)


def solution(mesh):
    in_specs = (
        P("bl", None, None),
        P("chan", "bl"),
        P(),
        P("chan", "bl", None),
        P("chan", "bl", None, None),
        P("chan", "bl", None, None),
        P("chan", "bl", None),
    )
    out_specs = (P("bl", "chan", None), P("chan", "bl", None, None))
    return jax.shard_map(shards, mesh=mesh, in_specs=in_specs, out_specs=out_specs, check_vma=False)
```

```python
import functools

import jax
import jax.numpy as jnp
from jax import lax
from jax.experimental import pallas as pl
from jax.experimental.pallas import tpu as pltpu
from jax.sharding import PartitionSpec as P

kernel_beta = 18.4
half_support = 4.0
step_length = 1.0
ridge_weight = 0.5


def spheroid(offset):
    scaled = offset * (1.0 / half_support)
    inside = scaled * scaled < 1.0
    root_term = jnp.sqrt(jnp.maximum(1.0 - scaled * scaled, 0.0))
    return jnp.where(inside, jnp.exp(kernel_beta * (root_term - 1.0)), 0.0)


def _spheroid_scaled(scaled):
    inside = scaled * scaled < 1.0
    rest = 1.0 - scaled * scaled
    root_term = rest * lax.rsqrt(rest)
    return jnp.where(inside, jnp.exp(kernel_beta * (root_term - 1.0)), 0.0)


def _grid_kernel(labels_ref, data_ref, tiles_ref, res_ref, grad_ref):
    slots = data_ref.shape[0]
    chunks, _, rows, _ = grad_ref.shape
    width = tiles_ref.shape[2]
    vis = data_ref.shape[2]
    grad_ref[...] = jnp.zeros(grad_ref.shape, grad_ref.dtype)
    cells = lax.broadcasted_iota(jnp.int32, (width, vis), 0).astype(jnp.float32) * (1.0 / half_support)

    def body(s, carry):
        d = data_ref[s]
        tile = labels_ref[s]
        quarter = d[3:5, :] * (1.0 / half_support)
        ku_t = _spheroid_scaled(cells - quarter[0:1]).astype(jnp.bfloat16)
        kv_t = _spheroid_scaled(cells - quarter[1:2]).astype(jnp.bfloat16).astype(jnp.float32)
        proj_t = jnp.dot(tiles_ref[tile], ku_t, preferred_element_type=jnp.float32)
        model_re = jnp.sum(proj_t[:width] * kv_t, axis=0, keepdims=True)
        model_im = jnp.sum(proj_t[width:] * kv_t, axis=0, keepdims=True)
        weight = d[2:3, :]
        res_re = weight * (model_re - d[0:1, :])
        res_im = weight * (model_im - d[1:2, :])
        res_ref[s] = jnp.concatenate([res_re, res_im], axis=0)
        spread_t = jnp.concatenate([res_re * kv_t, res_im * kv_t], axis=0).astype(jnp.bfloat16)
        contrib = lax.dot_general(
            ku_t, spread_t, (((1,), (1,)), ((), ())), preferred_element_type=jnp.float32
        )
        grad_ref[:, pl.ds(tile, 1)] += contrib.reshape(chunks, 1, rows, 2 * width)
        return carry

    lax.fori_loop(0, slots, body, 0, unroll=16)


def _grid_call(labels, data, tiles_t, chunks):
    slots, _, vis = data.shape
    tile_count, wide, width = tiles_t.shape
    vmem = pltpu.MemorySpace.VMEM
    return pl.pallas_call(
        _grid_kernel,
        out_shape=(
            jax.ShapeDtypeStruct((slots, 2, vis), jnp.float32),
            jax.ShapeDtypeStruct((chunks, tile_count, width // chunks, wide), jnp.float32),
        ),
        in_specs=[
            pl.BlockSpec(memory_space=pltpu.MemorySpace.SMEM),
            pl.BlockSpec(memory_space=vmem),
            pl.BlockSpec(memory_space=vmem),
        ],
        out_specs=(pl.BlockSpec(memory_space=vmem), pl.BlockSpec(memory_space=vmem)),
    )(labels, data, tiles_t)


def _ring_pairs(size_hi, size_lo, shift, along_lo):
    pairs = []
    for hi in range(size_hi):
        for lo in range(size_lo):
            if along_lo:
                pairs.append((hi * size_lo + lo, hi * size_lo + (lo + shift) % size_lo))
            else:
                pairs.append((hi * size_lo + lo, ((hi + shift) % size_hi) * size_lo + lo))
    return pairs


def _chan_reduce(gradient):
    chunks = gradient.shape[0]
    size_lo = 4
    size_hi = chunks // size_lo
    c = lax.axis_index("chan")
    hi, lo = c // size_lo, c % size_lo
    parts = gradient.reshape((size_hi, size_lo) + gradient.shape[1:])
    acc = lax.dynamic_index_in_dim(parts, lo, 1, keepdims=False)
    for k in range(1, size_lo):
        piece = lax.dynamic_index_in_dim(parts, (lo + k) % size_lo, 1, keepdims=False)
        acc = acc + lax.ppermute(piece, "chan", _ring_pairs(size_hi, size_lo, k, True))
    out = lax.dynamic_index_in_dim(acc, hi, 0, keepdims=False)
    for k in range(1, size_hi):
        piece = lax.dynamic_index_in_dim(acc, (hi + k) % size_hi, 0, keepdims=False)
        out = out + lax.ppermute(piece, "chan", _ring_pairs(size_hi, size_lo, k, False))
    return out


def shards(grid, tile_list, owner_map, offsets, positions, observed, weights):
    owners = lax.axis_size("bl")
    chan = lax.axis_size("chan")
    tile_dev = grid.shape[0]
    tile_width = grid.shape[1]
    block_count = tile_list.shape[1]
    capacity = 2 * block_count // owners
    slots_all = owners * capacity
    tile_ids = tile_list[0]
    slot_index = jnp.take(owner_map, tile_ids, axis=0)
    owner_index = slot_index // tile_dev
    local_slot = slot_index % tile_dev
    owner_onehot = (owner_index[:, None] == jnp.arange(owners, dtype=jnp.int32)[None, :]).astype(
        jnp.int32
    )
    earlier_count = jnp.cumsum(owner_onehot, axis=0) - owner_onehot
    place_rank = jnp.sum(owner_onehot * earlier_count, axis=1)
    send_slot = owner_index * capacity + place_rank
    coords = offsets[0].astype(jnp.float32)[..., None] + positions[0]
    vis = coords.shape[-1]
    label_row = jnp.broadcast_to(local_slot.astype(jnp.float32)[:, None, None], (block_count, 1, vis))
    payload = jnp.concatenate([observed[0], weights[0][:, None, :], coords, label_row], axis=1)
    match = send_slot[None, :] == jnp.arange(slots_all, dtype=jnp.int32)[:, None]
    source = jnp.sum(jnp.where(match, jnp.arange(block_count, dtype=jnp.int32)[None, :], 0), axis=1)
    filled = jnp.any(match, axis=1)
    outgoing = jnp.where(filled[:, None, None], jnp.take(payload, source, axis=0), 0.0)
    incoming = lax.all_to_all(outgoing, "bl", split_axis=0, concat_axis=0, tiled=True)
    labels = jnp.max(incoming[:, 5, :], axis=1).astype(jnp.int32)
    tiles_t = jnp.swapaxes(grid.astype(jnp.bfloat16), 1, 2)
    residual_all, gradient = _grid_call(labels, incoming, tiles_t, chan)
    share_rows = tile_width // chan
    grad_share = _chan_reduce(gradient)
    returned = lax.all_to_all(residual_all, "bl", split_axis=0, concat_axis=0, tiled=True)
    my_residual = jnp.take(returned, send_slot, axis=0)[None]
    share_start = lax.axis_index("chan") * share_rows
    own_rows = lax.dynamic_slice_in_dim(grid, share_start, share_rows, 1)
    new_grid = own_rows - step_length * (grad_share + ridge_weight * own_rows)
    return (new_grid, my_residual)


def solution(mesh):
    in_specs = (
        P("bl", None, None),
        P("chan", "bl"),
        P(),
        P("chan", "bl", None),
        P("chan", "bl", None, None),
        P("chan", "bl", None, None),
        P("chan", "bl", None),
    )
    out_specs = (P("bl", "chan", None), P("chan", "bl", None, None))
    return jax.shard_map(shards, mesh=mesh, in_specs=in_specs, out_specs=out_specs, check_vma=False)
```

```python
import functools

import jax
import jax.numpy as jnp
from jax import lax
from jax.experimental import pallas as pl
from jax.experimental.pallas import tpu as pltpu
from jax.sharding import PartitionSpec as P

kernel_beta = 18.4
half_support = 4.0
step_length = 1.0
ridge_weight = 0.5


def spheroid(offset):
    scaled = offset * (1.0 / half_support)
    inside = scaled * scaled < 1.0
    root_term = jnp.sqrt(jnp.maximum(1.0 - scaled * scaled, 0.0))
    return jnp.where(inside, jnp.exp(kernel_beta * (root_term - 1.0)), 0.0)


def _spheroid_scaled(scaled):
    inside = scaled * scaled < 1.0
    rest = 1.0 - scaled * scaled
    root_term = rest * lax.rsqrt(rest)
    return jnp.where(inside, jnp.exp(kernel_beta * (root_term - 1.0)), 0.0)


def _grid_kernel(labels_ref, data_ref, tiles_ref, res_ref, grad_ref):
    slots = data_ref.shape[0]
    chunks, _, rows, _ = grad_ref.shape
    width = tiles_ref.shape[2]
    vis = data_ref.shape[2]
    grad_ref[...] = jnp.zeros(grad_ref.shape, grad_ref.dtype)
    cells = lax.broadcasted_iota(jnp.int32, (width, vis), 0).astype(jnp.float32) * (1.0 / half_support)

    def body(s, carry):
        d = data_ref[s]
        tile = labels_ref[s]
        quarter = d[3:5, :] * (1.0 / half_support)
        ku_t = _spheroid_scaled(cells - quarter[0:1]).astype(jnp.bfloat16)
        kv_t = _spheroid_scaled(cells - quarter[1:2]).astype(jnp.bfloat16).astype(jnp.float32)
        proj_t = jnp.dot(tiles_ref[tile], ku_t, preferred_element_type=jnp.float32)
        model_re = jnp.sum(proj_t[:width] * kv_t, axis=0, keepdims=True)
        model_im = jnp.sum(proj_t[width:] * kv_t, axis=0, keepdims=True)
        weight = d[2:3, :]
        res_re = weight * (model_re - d[0:1, :])
        res_im = weight * (model_im - d[1:2, :])
        res_ref[s] = jnp.concatenate([res_re, res_im], axis=0)
        spread_t = jnp.concatenate([res_re * kv_t, res_im * kv_t], axis=0).astype(jnp.bfloat16)
        contrib = lax.dot_general(
            ku_t, spread_t, (((1,), (1,)), ((), ())), preferred_element_type=jnp.float32
        )
        grad_ref[:, pl.ds(tile, 1)] += contrib.reshape(chunks, 1, rows, 2 * width)
        return carry

    lax.fori_loop(0, slots, body, 0, unroll=16)


def _grid_call(labels, data, tiles_t, chunks):
    slots, _, vis = data.shape
    tile_count, wide, width = tiles_t.shape
    vmem = pltpu.MemorySpace.VMEM
    return pl.pallas_call(
        _grid_kernel,
        out_shape=(
            jax.ShapeDtypeStruct((slots, 2, vis), jnp.float32),
            jax.ShapeDtypeStruct((chunks, tile_count, width // chunks, wide), jnp.float32),
        ),
        in_specs=[
            pl.BlockSpec(memory_space=pltpu.MemorySpace.SMEM),
            pl.BlockSpec(memory_space=vmem),
            pl.BlockSpec(memory_space=vmem),
        ],
        out_specs=(pl.BlockSpec(memory_space=vmem), pl.BlockSpec(memory_space=vmem)),
    )(labels, data, tiles_t)


def _ring_pairs(size_hi, size_lo, shift, along_lo):
    pairs = []
    for hi in range(size_hi):
        for lo in range(size_lo):
            if along_lo:
                pairs.append((hi * size_lo + lo, hi * size_lo + (lo + shift) % size_lo))
            else:
                pairs.append((hi * size_lo + lo, ((hi + shift) % size_hi) * size_lo + lo))
    return pairs


def _chan_reduce(gradient):
    chunks = gradient.shape[0]
    size_lo = 4
    size_hi = chunks // size_lo
    c = lax.axis_index("chan")
    hi, lo = c // size_lo, c % size_lo
    parts = gradient.reshape((size_hi, size_lo) + gradient.shape[1:])
    acc = lax.dynamic_index_in_dim(parts, lo, 1, keepdims=False)
    for k in range(1, size_lo):
        piece = lax.dynamic_index_in_dim(parts, (lo + k) % size_lo, 1, keepdims=False)
        acc = acc + lax.ppermute(piece, "chan", _ring_pairs(size_hi, size_lo, k, True))
    for bit in (2, 1):
        halves = acc.reshape((2, acc.shape[0] // 2) + acc.shape[1:]) if bit == 2 else acc.reshape(
            (2, 1) + acc.shape[1:]
        )
        mine = (hi // bit) % 2
        keep = lax.dynamic_index_in_dim(halves, mine, 0, keepdims=False)
        give = lax.dynamic_index_in_dim(halves, 1 - mine, 0, keepdims=False)
        pairs = [
            (h * size_lo + l, (h ^ bit) * size_lo + l) for h in range(size_hi) for l in range(size_lo)
        ]
        acc = keep + lax.ppermute(give, "chan", pairs)
    return acc[0]


def shards(grid, tile_list, owner_map, offsets, positions, observed, weights):
    owners = lax.axis_size("bl")
    chan = lax.axis_size("chan")
    tile_dev = grid.shape[0]
    tile_width = grid.shape[1]
    block_count = tile_list.shape[1]
    capacity = 2 * block_count // owners
    slots_all = owners * capacity
    tile_ids = tile_list[0]
    slot_index = jnp.take(owner_map, tile_ids, axis=0)
    owner_index = slot_index // tile_dev
    local_slot = slot_index % tile_dev
    owner_onehot = (owner_index[:, None] == jnp.arange(owners, dtype=jnp.int32)[None, :]).astype(
        jnp.int32
    )
    earlier_count = jnp.cumsum(owner_onehot, axis=0) - owner_onehot
    place_rank = jnp.sum(owner_onehot * earlier_count, axis=1)
    send_slot = owner_index * capacity + place_rank
    coords = offsets[0].astype(jnp.float32)[..., None] + positions[0]
    vis = coords.shape[-1]
    label_row = jnp.broadcast_to(local_slot.astype(jnp.float32)[:, None, None], (block_count, 1, vis))
    payload = jnp.concatenate([observed[0], weights[0][:, None, :], coords, label_row], axis=1)
    match = send_slot[None, :] == jnp.arange(slots_all, dtype=jnp.int32)[:, None]
    source = jnp.sum(jnp.where(match, jnp.arange(block_count, dtype=jnp.int32)[None, :], 0), axis=1)
    filled = jnp.any(match, axis=1)
    outgoing = jnp.where(filled[:, None, None], jnp.take(payload, source, axis=0), 0.0)
    incoming = lax.all_to_all(outgoing, "bl", split_axis=0, concat_axis=0, tiled=True)
    labels = jnp.max(incoming[:, 5, :], axis=1).astype(jnp.int32)
    tiles_t = jnp.swapaxes(grid.astype(jnp.bfloat16), 1, 2)
    residual_all, gradient = _grid_call(labels, incoming, tiles_t, chan)
    share_rows = tile_width // chan
    grad_share = _chan_reduce(gradient)
    returned = lax.all_to_all(residual_all, "bl", split_axis=0, concat_axis=0, tiled=True)
    my_residual = jnp.take(returned, send_slot, axis=0)[None]
    share_start = lax.axis_index("chan") * share_rows
    own_rows = lax.dynamic_slice_in_dim(grid, share_start, share_rows, 1)
    new_grid = own_rows - step_length * (grad_share + ridge_weight * own_rows)
    return (new_grid, my_residual)


def solution(mesh):
    in_specs = (
        P("bl", None, None),
        P("chan", "bl"),
        P(),
        P("chan", "bl", None),
        P("chan", "bl", None, None),
        P("chan", "bl", None, None),
        P("chan", "bl", None),
    )
    out_specs = (P("bl", "chan", None), P("chan", "bl", None, None))
    return jax.shard_map(shards, mesh=mesh, in_specs=in_specs, out_specs=out_specs, check_vma=False)
```

```python
import functools

import jax
import jax.numpy as jnp
from jax import lax
from jax.experimental import pallas as pl
from jax.experimental.pallas import tpu as pltpu
from jax.sharding import PartitionSpec as P

kernel_beta = 18.4
half_support = 4.0
step_length = 1.0
ridge_weight = 0.5


def spheroid(offset):
    scaled = offset * (1.0 / half_support)
    inside = scaled * scaled < 1.0
    root_term = jnp.sqrt(jnp.maximum(1.0 - scaled * scaled, 0.0))
    return jnp.where(inside, jnp.exp(kernel_beta * (root_term - 1.0)), 0.0)


def _spheroid_scaled(scaled):
    inside = scaled * scaled < 1.0
    rest = 1.0 - scaled * scaled
    root_term = rest * lax.rsqrt(rest)
    return jnp.where(inside, jnp.exp(kernel_beta * (root_term - 1.0)), 0.0)


def _grid_kernel(labels_ref, data_ref, tiles_ref, res_ref, grad_ref):
    slots = data_ref.shape[0]
    chunks, _, rows, _ = grad_ref.shape
    width = tiles_ref.shape[2]
    vis = data_ref.shape[2]
    grad_ref[...] = jnp.zeros(grad_ref.shape, grad_ref.dtype)
    cells = lax.broadcasted_iota(jnp.int32, (width, vis), 0).astype(jnp.float32) * (1.0 / half_support)

    def body(s, carry):
        d = data_ref[s]
        tile = labels_ref[s]
        quarter = d[3:5, :] * (1.0 / half_support)
        ku_t = _spheroid_scaled(cells - quarter[0:1]).astype(jnp.bfloat16)
        kv_t = _spheroid_scaled(cells - quarter[1:2]).astype(jnp.bfloat16).astype(jnp.float32)
        proj_t = jnp.dot(tiles_ref[tile], ku_t, preferred_element_type=jnp.float32)
        model_re = jnp.sum(proj_t[:width] * kv_t, axis=0, keepdims=True)
        model_im = jnp.sum(proj_t[width:] * kv_t, axis=0, keepdims=True)
        weight = d[2:3, :]
        res_re = weight * (model_re - d[0:1, :])
        res_im = weight * (model_im - d[1:2, :])
        res_ref[s] = jnp.concatenate([res_re, res_im], axis=0)
        spread_t = jnp.concatenate([res_re * kv_t, res_im * kv_t], axis=0).astype(jnp.bfloat16)
        contrib = lax.dot_general(
            ku_t, spread_t, (((1,), (1,)), ((), ())), preferred_element_type=jnp.float32
        )
        grad_ref[:, pl.ds(tile, 1)] += contrib.reshape(chunks, 1, rows, 2 * width)
        return carry

    lax.fori_loop(0, slots, body, 0, unroll=16)


def _grid_call(labels, data, tiles_t, chunks):
    slots, _, vis = data.shape
    tile_count, wide, width = tiles_t.shape
    vmem = pltpu.MemorySpace.VMEM
    return pl.pallas_call(
        _grid_kernel,
        out_shape=(
            jax.ShapeDtypeStruct((slots, 2, vis), jnp.float32),
            jax.ShapeDtypeStruct((chunks, tile_count, width // chunks, wide), jnp.float32),
        ),
        in_specs=[
            pl.BlockSpec(memory_space=pltpu.MemorySpace.SMEM),
            pl.BlockSpec(memory_space=vmem),
            pl.BlockSpec(memory_space=vmem),
        ],
        out_specs=(pl.BlockSpec(memory_space=vmem), pl.BlockSpec(memory_space=vmem)),
    )(labels, data, tiles_t)


def _ring_pairs(size_hi, size_lo, shift, along_lo):
    pairs = []
    for hi in range(size_hi):
        for lo in range(size_lo):
            if along_lo:
                pairs.append((hi * size_lo + lo, hi * size_lo + (lo + shift) % size_lo))
            else:
                pairs.append((hi * size_lo + lo, ((hi + shift) % size_hi) * size_lo + lo))
    return pairs


def _chan_reduce(gradient):
    chunks = gradient.shape[0]
    size_lo = 4
    size_hi = chunks // size_lo
    c = lax.axis_index("chan")
    hi, lo = c // size_lo, c % size_lo
    parts = gradient.reshape((size_hi, size_lo) + gradient.shape[1:])
    acc = lax.dynamic_index_in_dim(parts, lo, 1, keepdims=False)
    for k in range(1, size_lo):
        piece = lax.dynamic_index_in_dim(parts, (lo + k) % size_lo, 1, keepdims=False)
        acc = acc + lax.ppermute(piece, "chan", _ring_pairs(size_hi, size_lo, k, True))
    for bit in (1, 2):
        axis = 1 if bit == 1 else 0
        halves = acc.reshape((2, acc.shape[0] // 2) + acc.shape[1:]) if bit == 1 else acc
        mine = (hi // bit) % 2
        keep = lax.dynamic_index_in_dim(halves, mine, axis, keepdims=False)
        give = lax.dynamic_index_in_dim(halves, 1 - mine, axis, keepdims=False)
        pairs = [
            (h * size_lo + l, (h ^ bit) * size_lo + l) for h in range(size_hi) for l in range(size_lo)
        ]
        acc = keep + lax.ppermute(give, "chan", pairs)
    return acc


def shards(grid, tile_list, owner_map, offsets, positions, observed, weights):
    owners = lax.axis_size("bl")
    chan = lax.axis_size("chan")
    tile_dev = grid.shape[0]
    tile_width = grid.shape[1]
    block_count = tile_list.shape[1]
    capacity = 2 * block_count // owners
    slots_all = owners * capacity
    tile_ids = tile_list[0]
    slot_index = jnp.take(owner_map, tile_ids, axis=0)
    owner_index = slot_index // tile_dev
    local_slot = slot_index % tile_dev
    owner_onehot = (owner_index[:, None] == jnp.arange(owners, dtype=jnp.int32)[None, :]).astype(
        jnp.int32
    )
    earlier_count = jnp.cumsum(owner_onehot, axis=0) - owner_onehot
    place_rank = jnp.sum(owner_onehot * earlier_count, axis=1)
    send_slot = owner_index * capacity + place_rank
    coords = offsets[0].astype(jnp.float32)[..., None] + positions[0]
    vis = coords.shape[-1]
    label_row = jnp.broadcast_to(local_slot.astype(jnp.float32)[:, None, None], (block_count, 1, vis))
    payload = jnp.concatenate([observed[0], weights[0][:, None, :], coords, label_row], axis=1)
    match = send_slot[None, :] == jnp.arange(slots_all, dtype=jnp.int32)[:, None]
    source = jnp.sum(jnp.where(match, jnp.arange(block_count, dtype=jnp.int32)[None, :], 0), axis=1)
    filled = jnp.any(match, axis=1)
    outgoing = jnp.where(filled[:, None, None], jnp.take(payload, source, axis=0), 0.0)
    incoming = lax.all_to_all(outgoing, "bl", split_axis=0, concat_axis=0, tiled=True)
    labels = jnp.max(incoming[:, 5, :], axis=1).astype(jnp.int32)
    tiles_t = jnp.swapaxes(grid.astype(jnp.bfloat16), 1, 2)
    residual_all, gradient = _grid_call(labels, incoming, tiles_t, chan)
    share_rows = tile_width // chan
    grad_share = _chan_reduce(gradient)
    returned = lax.all_to_all(residual_all, "bl", split_axis=0, concat_axis=0, tiled=True)
    my_residual = jnp.take(returned, send_slot, axis=0)[None]
    share_start = lax.axis_index("chan") * share_rows
    own_rows = lax.dynamic_slice_in_dim(grid, share_start, share_rows, 1)
    new_grid = own_rows - step_length * (grad_share + ridge_weight * own_rows)
    return (new_grid, my_residual)


def solution(mesh):
    in_specs = (
        P("bl", None, None),
        P("chan", "bl"),
        P(),
        P("chan", "bl", None),
        P("chan", "bl", None, None),
        P("chan", "bl", None, None),
        P("chan", "bl", None),
    )
    out_specs = (P("bl", "chan", None), P("chan", "bl", None, None))
    return jax.shard_map(shards, mesh=mesh, in_specs=in_specs, out_specs=out_specs, check_vma=False)
```

```python
import functools

import jax
import jax.numpy as jnp
from jax import lax
from jax.experimental import pallas as pl
from jax.experimental.pallas import tpu as pltpu
from jax.sharding import PartitionSpec as P

kernel_beta = 18.4
half_support = 4.0
step_length = 1.0
ridge_weight = 0.5


def spheroid(offset):
    scaled = offset * (1.0 / half_support)
    inside = scaled * scaled < 1.0
    root_term = jnp.sqrt(jnp.maximum(1.0 - scaled * scaled, 0.0))
    return jnp.where(inside, jnp.exp(kernel_beta * (root_term - 1.0)), 0.0)


def _spheroid_scaled(scaled):
    inside = scaled * scaled < 1.0
    rest = 1.0 - scaled * scaled
    root_term = rest * lax.rsqrt(rest)
    return jnp.where(inside, jnp.exp(kernel_beta * (root_term - 1.0)), 0.0)


def _grid_kernel(labels_ref, data_ref, tiles_ref, res_ref, grad_ref):
    slots = data_ref.shape[0]
    chunks, _, rows, _ = grad_ref.shape
    width = tiles_ref.shape[2]
    vis = data_ref.shape[2]
    grad_ref[...] = jnp.zeros(grad_ref.shape, grad_ref.dtype)
    cells = lax.broadcasted_iota(jnp.int32, (width, vis), 0).astype(jnp.float32) * (1.0 / half_support)

    def body(s, carry):
        d = data_ref[s]
        tile = labels_ref[s]
        quarter = d[3:5, :] * (1.0 / half_support)
        ku_t = _spheroid_scaled(cells - quarter[0:1]).astype(jnp.bfloat16)
        kv_t = _spheroid_scaled(cells - quarter[1:2]).astype(jnp.bfloat16).astype(jnp.float32)
        proj_t = jnp.dot(tiles_ref[tile], ku_t, preferred_element_type=jnp.float32)
        model_re = jnp.sum(proj_t[:width] * kv_t, axis=0, keepdims=True)
        model_im = jnp.sum(proj_t[width:] * kv_t, axis=0, keepdims=True)
        weight = d[2:3, :]
        res_re = weight * (model_re - d[0:1, :])
        res_im = weight * (model_im - d[1:2, :])
        res_ref[s] = jnp.concatenate([res_re, res_im], axis=0)
        spread_t = jnp.concatenate([res_re * kv_t, res_im * kv_t], axis=0).astype(jnp.bfloat16)
        contrib = lax.dot_general(
            ku_t, spread_t, (((1,), (1,)), ((), ())), preferred_element_type=jnp.float32
        )
        grad_ref[:, pl.ds(tile, 1)] += contrib.reshape(chunks, 1, rows, 2 * width)
        return carry

    lax.fori_loop(0, slots, body, 0, unroll=16)


def _grid_call(labels, data, tiles_t, chunks):
    slots, _, vis = data.shape
    tile_count, wide, width = tiles_t.shape
    vmem = pltpu.MemorySpace.VMEM
    return pl.pallas_call(
        _grid_kernel,
        out_shape=(
            jax.ShapeDtypeStruct((slots, 2, vis), jnp.float32),
            jax.ShapeDtypeStruct((chunks, tile_count, width // chunks, wide), jnp.float32),
        ),
        in_specs=[
            pl.BlockSpec(memory_space=pltpu.MemorySpace.SMEM),
            pl.BlockSpec(memory_space=vmem),
            pl.BlockSpec(memory_space=vmem),
        ],
        out_specs=(pl.BlockSpec(memory_space=vmem), pl.BlockSpec(memory_space=vmem)),
    )(labels, data, tiles_t)


def _chan_reduce(gradient):
    chunks = gradient.shape[0]
    size_lo = 4
    size_hi = chunks // size_lo
    c = lax.axis_index("chan")
    hi, lo = c // size_lo, c % size_lo
    acc = gradient.reshape((size_hi, 2, 2) + gradient.shape[1:])
    for bit in (2, 1):
        mine = (lo // bit) % 2
        keep = lax.dynamic_index_in_dim(acc, mine, 1, keepdims=False)
        give = lax.dynamic_index_in_dim(acc, 1 - mine, 1, keepdims=False)
        pairs = [
            (h * size_lo + l, h * size_lo + (l ^ bit)) for h in range(size_hi) for l in range(size_lo)
        ]
        acc = keep + lax.ppermute(give, "chan", pairs)
    for bit in (2, 1):
        halves = acc.reshape((2, acc.shape[0] // 2) + acc.shape[1:]) if bit == 2 else acc.reshape(
            (2, 1) + acc.shape[1:]
        )
        mine = (hi // bit) % 2
        keep = lax.dynamic_index_in_dim(halves, mine, 0, keepdims=False)
        give = lax.dynamic_index_in_dim(halves, 1 - mine, 0, keepdims=False)
        pairs = [
            (h * size_lo + l, (h ^ bit) * size_lo + l) for h in range(size_hi) for l in range(size_lo)
        ]
        acc = keep + lax.ppermute(give, "chan", pairs)
    return acc[0]


def shards(grid, tile_list, owner_map, offsets, positions, observed, weights):
    owners = lax.axis_size("bl")
    chan = lax.axis_size("chan")
    tile_dev = grid.shape[0]
    tile_width = grid.shape[1]
    block_count = tile_list.shape[1]
    capacity = 2 * block_count // owners
    slots_all = owners * capacity
    tile_ids = tile_list[0]
    slot_index = jnp.take(owner_map, tile_ids, axis=0)
    owner_index = slot_index // tile_dev
    local_slot = slot_index % tile_dev
    owner_onehot = (owner_index[:, None] == jnp.arange(owners, dtype=jnp.int32)[None, :]).astype(
        jnp.int32
    )
    earlier_count = jnp.cumsum(owner_onehot, axis=0) - owner_onehot
    place_rank = jnp.sum(owner_onehot * earlier_count, axis=1)
    send_slot = owner_index * capacity + place_rank
    coords = offsets[0].astype(jnp.float32)[..., None] + positions[0]
    vis = coords.shape[-1]
    label_row = jnp.broadcast_to(local_slot.astype(jnp.float32)[:, None, None], (block_count, 1, vis))
    payload = jnp.concatenate([observed[0], weights[0][:, None, :], coords, label_row], axis=1)
    match = send_slot[None, :] == jnp.arange(slots_all, dtype=jnp.int32)[:, None]
    source = jnp.sum(jnp.where(match, jnp.arange(block_count, dtype=jnp.int32)[None, :], 0), axis=1)
    filled = jnp.any(match, axis=1)
    outgoing = jnp.where(filled[:, None, None], jnp.take(payload, source, axis=0), 0.0)
    incoming = lax.all_to_all(outgoing, "bl", split_axis=0, concat_axis=0, tiled=True)
    labels = jnp.max(incoming[:, 5, :], axis=1).astype(jnp.int32)
    tiles_t = jnp.swapaxes(grid.astype(jnp.bfloat16), 1, 2)
    residual_all, gradient = _grid_call(labels, incoming, tiles_t, chan)
    share_rows = tile_width // chan
    grad_share = _chan_reduce(gradient)
    returned = lax.all_to_all(residual_all, "bl", split_axis=0, concat_axis=0, tiled=True)
    my_residual = jnp.take(returned, send_slot, axis=0)[None]
    share_start = lax.axis_index("chan") * share_rows
    own_rows = lax.dynamic_slice_in_dim(grid, share_start, share_rows, 1)
    new_grid = own_rows - step_length * (grad_share + ridge_weight * own_rows)
    return (new_grid, my_residual)


def solution(mesh):
    in_specs = (
        P("bl", None, None),
        P("chan", "bl"),
        P(),
        P("chan", "bl", None),
        P("chan", "bl", None, None),
        P("chan", "bl", None, None),
        P("chan", "bl", None),
    )
    out_specs = (P("bl", "chan", None), P("chan", "bl", None, None))
    return jax.shard_map(shards, mesh=mesh, in_specs=in_specs, out_specs=out_specs, check_vma=False)
```

```python
import functools

import jax
import jax.numpy as jnp
from jax import lax
from jax.experimental import pallas as pl
from jax.experimental.pallas import tpu as pltpu
from jax.sharding import PartitionSpec as P

kernel_beta = 18.4
half_support = 4.0
step_length = 1.0
ridge_weight = 0.5


def spheroid(offset):
    scaled = offset * (1.0 / half_support)
    inside = scaled * scaled < 1.0
    root_term = jnp.sqrt(jnp.maximum(1.0 - scaled * scaled, 0.0))
    return jnp.where(inside, jnp.exp(kernel_beta * (root_term - 1.0)), 0.0)


def _spheroid_scaled(scaled):
    inside = scaled * scaled < 1.0
    rest = 1.0 - scaled * scaled
    root_term = rest * lax.rsqrt(rest)
    return jnp.where(inside, jnp.exp(kernel_beta * (root_term - 1.0)), 0.0)


def _grid_kernel(labels_ref, data_ref, tiles_ref, res_ref, grad_ref):
    slots = data_ref.shape[0]
    chunks, _, rows, _ = grad_ref.shape
    width = tiles_ref.shape[2]
    vis = data_ref.shape[2]
    grad_ref[...] = jnp.zeros(grad_ref.shape, grad_ref.dtype)
    cells = lax.broadcasted_iota(jnp.int32, (width, vis), 0).astype(jnp.float32) * (1.0 / half_support)

    def body(s, carry):
        d = data_ref[s]
        tile = labels_ref[s]
        quarter = d[3:5, :] * (1.0 / half_support)
        ku_t = _spheroid_scaled(cells - quarter[0:1]).astype(jnp.bfloat16)
        kv_t = _spheroid_scaled(cells - quarter[1:2]).astype(jnp.bfloat16).astype(jnp.float32)
        proj_t = jnp.dot(tiles_ref[tile], ku_t, preferred_element_type=jnp.float32)
        model_re = jnp.sum(proj_t[:width] * kv_t, axis=0, keepdims=True)
        model_im = jnp.sum(proj_t[width:] * kv_t, axis=0, keepdims=True)
        weight = d[2:3, :]
        res_re = weight * (model_re - d[0:1, :])
        res_im = weight * (model_im - d[1:2, :])
        res_ref[s] = jnp.concatenate([res_re, res_im], axis=0)
        spread_t = jnp.concatenate([res_re * kv_t, res_im * kv_t], axis=0).astype(jnp.bfloat16)
        contrib = lax.dot_general(
            ku_t, spread_t, (((1,), (1,)), ((), ())), preferred_element_type=jnp.float32
        )
        grad_ref[:, pl.ds(tile, 1)] += contrib.reshape(chunks, 1, rows, 2 * width)
        return carry

    lax.fori_loop(0, slots, body, 0, unroll=32)


def _grid_call(labels, data, tiles_t, chunks):
    slots, _, vis = data.shape
    tile_count, wide, width = tiles_t.shape
    vmem = pltpu.MemorySpace.VMEM
    return pl.pallas_call(
        _grid_kernel,
        out_shape=(
            jax.ShapeDtypeStruct((slots, 2, vis), jnp.float32),
            jax.ShapeDtypeStruct((chunks, tile_count, width // chunks, wide), jnp.float32),
        ),
        in_specs=[
            pl.BlockSpec(memory_space=pltpu.MemorySpace.SMEM),
            pl.BlockSpec(memory_space=vmem),
            pl.BlockSpec(memory_space=vmem),
        ],
        out_specs=(pl.BlockSpec(memory_space=vmem), pl.BlockSpec(memory_space=vmem)),
    )(labels, data, tiles_t)


def _ring_pairs(size_hi, size_lo, shift, along_lo):
    pairs = []
    for hi in range(size_hi):
        for lo in range(size_lo):
            if along_lo:
                pairs.append((hi * size_lo + lo, hi * size_lo + (lo + shift) % size_lo))
            else:
                pairs.append((hi * size_lo + lo, ((hi + shift) % size_hi) * size_lo + lo))
    return pairs


def _chan_reduce(gradient):
    chunks = gradient.shape[0]
    size_lo = 4
    size_hi = chunks // size_lo
    c = lax.axis_index("chan")
    hi, lo = c // size_lo, c % size_lo
    parts = gradient.reshape((size_hi, size_lo) + gradient.shape[1:])
    acc = lax.dynamic_index_in_dim(parts, lo, 1, keepdims=False)
    for k in range(1, size_lo):
        piece = lax.dynamic_index_in_dim(parts, (lo + k) % size_lo, 1, keepdims=False)
        acc = acc + lax.ppermute(piece, "chan", _ring_pairs(size_hi, size_lo, k, True))
    for bit in (2, 1):
        halves = acc.reshape((2, acc.shape[0] // 2) + acc.shape[1:]) if bit == 2 else acc.reshape(
            (2, 1) + acc.shape[1:]
        )
        mine = (hi // bit) % 2
        keep = lax.dynamic_index_in_dim(halves, mine, 0, keepdims=False)
        give = lax.dynamic_index_in_dim(halves, 1 - mine, 0, keepdims=False)
        pairs = [
            (h * size_lo + l, (h ^ bit) * size_lo + l) for h in range(size_hi) for l in range(size_lo)
        ]
        acc = keep + lax.ppermute(give, "chan", pairs)
    return acc[0]


def shards(grid, tile_list, owner_map, offsets, positions, observed, weights):
    owners = lax.axis_size("bl")
    chan = lax.axis_size("chan")
    tile_dev = grid.shape[0]
    tile_width = grid.shape[1]
    block_count = tile_list.shape[1]
    capacity = 2 * block_count // owners
    slots_all = owners * capacity
    tile_ids = tile_list[0]
    slot_index = jnp.take(owner_map, tile_ids, axis=0)
    owner_index = slot_index // tile_dev
    local_slot = slot_index % tile_dev
    owner_onehot = (owner_index[:, None] == jnp.arange(owners, dtype=jnp.int32)[None, :]).astype(
        jnp.int32
    )
    earlier_count = jnp.cumsum(owner_onehot, axis=0) - owner_onehot
    place_rank = jnp.sum(owner_onehot * earlier_count, axis=1)
    send_slot = owner_index * capacity + place_rank
    coords = offsets[0].astype(jnp.float32)[..., None] + positions[0]
    vis = coords.shape[-1]
    label_row = jnp.broadcast_to(local_slot.astype(jnp.float32)[:, None, None], (block_count, 1, vis))
    payload = jnp.concatenate([observed[0], weights[0][:, None, :], coords, label_row], axis=1)
    match = send_slot[None, :] == jnp.arange(slots_all, dtype=jnp.int32)[:, None]
    source = jnp.sum(jnp.where(match, jnp.arange(block_count, dtype=jnp.int32)[None, :], 0), axis=1)
    source = jnp.where(jnp.any(match, axis=1), source, block_count)
    padded = jnp.concatenate([payload, jnp.zeros((1,) + payload.shape[1:], payload.dtype)], axis=0)
    outgoing = jnp.take(padded, source, axis=0)
    incoming = lax.all_to_all(outgoing, "bl", split_axis=0, concat_axis=0, tiled=True)
    labels = jnp.max(incoming[:, 5, :].astype(jnp.int32), axis=1)
    tiles_t = jnp.swapaxes(grid.astype(jnp.bfloat16), 1, 2)
    residual_all, gradient = _grid_call(labels, incoming, tiles_t, chan)
    share_rows = tile_width // chan
    grad_share = _chan_reduce(gradient)
    returned = lax.all_to_all(residual_all, "bl", split_axis=0, concat_axis=0, tiled=True)
    my_residual = jnp.take(returned, send_slot, axis=0)[None]
    share_start = lax.axis_index("chan") * share_rows
    own_rows = lax.dynamic_slice_in_dim(grid, share_start, share_rows, 1)
    new_grid = own_rows - step_length * (grad_share + ridge_weight * own_rows)
    return (new_grid, my_residual)


def solution(mesh):
    in_specs = (
        P("bl", None, None),
        P("chan", "bl"),
        P(),
        P("chan", "bl", None),
        P("chan", "bl", None, None),
        P("chan", "bl", None, None),
        P("chan", "bl", None),
    )
    out_specs = (P("bl", "chan", None), P("chan", "bl", None, None))
    return jax.shard_map(shards, mesh=mesh, in_specs=in_specs, out_specs=out_specs, check_vma=False)
```

```python
import functools

import jax
import jax.numpy as jnp
from jax import lax
from jax.experimental import pallas as pl
from jax.experimental.pallas import tpu as pltpu
from jax.sharding import PartitionSpec as P

kernel_beta = 18.4
half_support = 4.0
step_length = 1.0
ridge_weight = 0.5


def spheroid(offset):
    scaled = offset * (1.0 / half_support)
    inside = scaled * scaled < 1.0
    root_term = jnp.sqrt(jnp.maximum(1.0 - scaled * scaled, 0.0))
    return jnp.where(inside, jnp.exp(kernel_beta * (root_term - 1.0)), 0.0)


def _spheroid_scaled(scaled):
    inside = scaled * scaled < 1.0
    rest = 1.0 - scaled * scaled
    root_term = rest * lax.rsqrt(rest)
    return jnp.where(inside, jnp.exp(kernel_beta * (root_term - 1.0)), 0.0)


def _grid_kernel(labels_ref, data_ref, tiles_ref, res_ref, grad_ref):
    slots = data_ref.shape[0]
    chunks, _, rows, _ = grad_ref.shape
    width = tiles_ref.shape[2]
    vis = data_ref.shape[2]
    grad_ref[...] = jnp.zeros(grad_ref.shape, grad_ref.dtype)
    cells = lax.broadcasted_iota(jnp.int32, (width, vis), 0).astype(jnp.float32) * (1.0 / half_support)

    def body(s, carry):
        d = data_ref[s]
        tile = labels_ref[s]
        quarter = d[3:5, :] * (1.0 / half_support)
        ku_t = _spheroid_scaled(cells - quarter[0:1]).astype(jnp.bfloat16)
        kv_t = _spheroid_scaled(cells - quarter[1:2]).astype(jnp.bfloat16).astype(jnp.float32)
        proj_t = jnp.dot(tiles_ref[tile], ku_t, preferred_element_type=jnp.float32)
        model_re = jnp.sum(proj_t[:width] * kv_t, axis=0, keepdims=True)
        model_im = jnp.sum(proj_t[width:] * kv_t, axis=0, keepdims=True)
        weight = d[2:3, :]
        res_re = weight * (model_re - d[0:1, :])
        res_im = weight * (model_im - d[1:2, :])
        res_ref[s] = jnp.concatenate([res_re, res_im], axis=0)
        spread_t = jnp.concatenate([res_re * kv_t, res_im * kv_t], axis=0).astype(jnp.bfloat16)
        contrib = lax.dot_general(
            ku_t, spread_t, (((1,), (1,)), ((), ())), preferred_element_type=jnp.float32
        )
        grad_ref[:, pl.ds(tile, 1)] += contrib.reshape(chunks, 1, rows, 2 * width)
        return carry

    lax.fori_loop(0, slots, body, 0, unroll=32)


def _grid_call(labels, data, tiles_t, chunks):
    slots, _, vis = data.shape
    tile_count, wide, width = tiles_t.shape
    vmem = pltpu.MemorySpace.VMEM
    return pl.pallas_call(
        _grid_kernel,
        out_shape=(
            jax.ShapeDtypeStruct((slots, 2, vis), jnp.float32),
            jax.ShapeDtypeStruct((chunks, tile_count, width // chunks, wide), jnp.float32),
        ),
        in_specs=[
            pl.BlockSpec(memory_space=pltpu.MemorySpace.SMEM),
            pl.BlockSpec(memory_space=vmem),
            pl.BlockSpec(memory_space=vmem),
        ],
        out_specs=(pl.BlockSpec(memory_space=vmem), pl.BlockSpec(memory_space=vmem)),
    )(labels, data, tiles_t)


def _ring_pairs(size_hi, size_lo, shift, along_lo):
    pairs = []
    for hi in range(size_hi):
        for lo in range(size_lo):
            if along_lo:
                pairs.append((hi * size_lo + lo, hi * size_lo + (lo + shift) % size_lo))
            else:
                pairs.append((hi * size_lo + lo, ((hi + shift) % size_hi) * size_lo + lo))
    return pairs


def _chan_reduce(gradient):
    chunks = gradient.shape[0]
    size_lo = 4
    size_hi = chunks // size_lo
    c = lax.axis_index("chan")
    hi, lo = c // size_lo, c % size_lo
    parts = gradient.reshape((size_hi, size_lo) + gradient.shape[1:])
    acc = lax.dynamic_index_in_dim(parts, lo, 1, keepdims=False)
    for k in range(1, size_lo):
        piece = lax.dynamic_index_in_dim(parts, (lo + k) % size_lo, 1, keepdims=False)
        acc = acc + lax.ppermute(piece, "chan", _ring_pairs(size_hi, size_lo, k, True))
    for bit in (2, 1):
        halves = acc.reshape((2, acc.shape[0] // 2) + acc.shape[1:]) if bit == 2 else acc.reshape(
            (2, 1) + acc.shape[1:]
        )
        mine = (hi // bit) % 2
        keep = lax.dynamic_index_in_dim(halves, mine, 0, keepdims=False)
        give = lax.dynamic_index_in_dim(halves, 1 - mine, 0, keepdims=False)
        pairs = [
            (h * size_lo + l, (h ^ bit) * size_lo + l) for h in range(size_hi) for l in range(size_lo)
        ]
        acc = keep + lax.ppermute(give, "chan", pairs)
    return acc[0]


def shards(grid, tile_list, owner_map, offsets, positions, observed, weights):
    owners = lax.axis_size("bl")
    chan = lax.axis_size("chan")
    tile_dev = grid.shape[0]
    tile_width = grid.shape[1]
    block_count = tile_list.shape[1]
    capacity = 2 * block_count // owners
    slots_all = owners * capacity
    tile_ids = tile_list[0]
    slot_index = jnp.take(owner_map, tile_ids, axis=0)
    owner_index = slot_index // tile_dev
    local_slot = slot_index % tile_dev
    owner_onehot = (owner_index[:, None] == jnp.arange(owners, dtype=jnp.int32)[None, :]).astype(
        jnp.int32
    )
    earlier_count = jnp.cumsum(owner_onehot, axis=0) - owner_onehot
    place_rank = jnp.sum(owner_onehot * earlier_count, axis=1)
    send_slot = owner_index * capacity + place_rank
    coords = offsets[0].astype(jnp.float32)[..., None] + positions[0]
    vis = coords.shape[-1]
    label_row = jnp.broadcast_to(local_slot.astype(jnp.float32)[:, None, None], (block_count, 1, vis))
    payload = jnp.concatenate([observed[0], weights[0][:, None, :], coords, label_row], axis=1)
    match = send_slot[None, :] == jnp.arange(slots_all, dtype=jnp.int32)[:, None]
    source = jnp.sum(jnp.where(match, jnp.arange(block_count, dtype=jnp.int32)[None, :], 0), axis=1)
    source = jnp.where(jnp.any(match, axis=1), source, block_count)
    padded = jnp.concatenate([payload, jnp.zeros((1,) + payload.shape[1:], payload.dtype)], axis=0)
    outgoing = jnp.take(padded, source, axis=0)
    incoming = lax.all_to_all(outgoing, "bl", split_axis=0, concat_axis=0, tiled=True)
    labels = jnp.max(incoming[:, 5, :], axis=1).astype(jnp.int32)
    tiles_t = jnp.swapaxes(grid.astype(jnp.bfloat16), 1, 2)
    residual_all, gradient = _grid_call(labels, incoming, tiles_t, chan)
    share_rows = tile_width // chan
    grad_share = _chan_reduce(gradient)
    returned = lax.all_to_all(residual_all, "bl", split_axis=0, concat_axis=0, tiled=True)
    my_residual = jnp.take(returned, send_slot, axis=0)[None]
    share_start = lax.axis_index("chan") * share_rows
    own_rows = lax.dynamic_slice_in_dim(grid, share_start, share_rows, 1)
    new_grid = own_rows - step_length * (grad_share + ridge_weight * own_rows)
    return (new_grid, my_residual)


def solution(mesh):
    in_specs = (
        P("bl", None, None),
        P("chan", "bl"),
        P(),
        P("chan", "bl", None),
        P("chan", "bl", None, None),
        P("chan", "bl", None, None),
        P("chan", "bl", None),
    )
    out_specs = (P("bl", "chan", None), P("chan", "bl", None, None))
    return jax.shard_map(shards, mesh=mesh, in_specs=in_specs, out_specs=out_specs, check_vma=False)
```

```python
import functools

import jax
import jax.numpy as jnp
from jax import lax
from jax.experimental import pallas as pl
from jax.experimental.pallas import tpu as pltpu
from jax.sharding import PartitionSpec as P

kernel_beta = 18.4
half_support = 4.0
step_length = 1.0
ridge_weight = 0.5


def spheroid(offset):
    scaled = offset * (1.0 / half_support)
    inside = scaled * scaled < 1.0
    root_term = jnp.sqrt(jnp.maximum(1.0 - scaled * scaled, 0.0))
    return jnp.where(inside, jnp.exp(kernel_beta * (root_term - 1.0)), 0.0)


def _spheroid_scaled(scaled):
    inside = scaled * scaled < 1.0
    rest = 1.0 - scaled * scaled
    root_term = rest * lax.rsqrt(rest)
    return jnp.where(inside, jnp.exp(kernel_beta * (root_term - 1.0)), 0.0)


def _grid_kernel(labels_ref, data_ref, tiles_ref, res_ref, grad_ref):
    slots = data_ref.shape[0]
    chunks, _, rows, _ = grad_ref.shape
    width = tiles_ref.shape[2]
    vis = data_ref.shape[2]
    grad_ref[...] = jnp.zeros(grad_ref.shape, grad_ref.dtype)
    cells = lax.broadcasted_iota(jnp.int32, (width, vis), 0).astype(jnp.float32) * (1.0 / half_support)

    def body(s, carry):
        d = data_ref[s]
        tile = labels_ref[s]
        quarter = d[3:5, :] * (1.0 / half_support)
        ku_t = _spheroid_scaled(cells - quarter[0:1]).astype(jnp.bfloat16)
        kv_t = _spheroid_scaled(cells - quarter[1:2]).astype(jnp.bfloat16).astype(jnp.float32)
        proj_t = jnp.dot(tiles_ref[tile], ku_t, preferred_element_type=jnp.float32)
        model_re = jnp.sum(proj_t[:width] * kv_t, axis=0, keepdims=True)
        model_im = jnp.sum(proj_t[width:] * kv_t, axis=0, keepdims=True)
        weight = d[2:3, :]
        res_re = weight * (model_re - d[0:1, :])
        res_im = weight * (model_im - d[1:2, :])
        res_ref[s] = jnp.concatenate([res_re, res_im], axis=0)
        spread_t = jnp.concatenate([res_re * kv_t, res_im * kv_t], axis=0).astype(jnp.bfloat16)
        contrib = lax.dot_general(
            ku_t, spread_t, (((1,), (1,)), ((), ())), preferred_element_type=jnp.float32
        )
        grad_ref[:, pl.ds(tile, 1)] += contrib.reshape(chunks, 1, rows, 2 * width)
        return carry

    lax.fori_loop(0, slots, body, 0, unroll=32)


def _grid_call(labels, data, tiles_t, chunks):
    slots, _, vis = data.shape
    tile_count, wide, width = tiles_t.shape
    vmem = pltpu.MemorySpace.VMEM
    return pl.pallas_call(
        _grid_kernel,
        out_shape=(
            jax.ShapeDtypeStruct((slots, 2, vis), jnp.float32),
            jax.ShapeDtypeStruct((chunks, tile_count, width // chunks, wide), jnp.float32),
        ),
        in_specs=[
            pl.BlockSpec(memory_space=pltpu.MemorySpace.SMEM),
            pl.BlockSpec(memory_space=vmem),
            pl.BlockSpec(memory_space=vmem),
        ],
        out_specs=(pl.BlockSpec(memory_space=vmem), pl.BlockSpec(memory_space=vmem)),
    )(labels, data, tiles_t)


def _ring_pairs(size_hi, size_lo, shift, along_lo):
    pairs = []
    for hi in range(size_hi):
        for lo in range(size_lo):
            if along_lo:
                pairs.append((hi * size_lo + lo, hi * size_lo + (lo + shift) % size_lo))
            else:
                pairs.append((hi * size_lo + lo, ((hi + shift) % size_hi) * size_lo + lo))
    return pairs


def _chan_reduce(gradient):
    chunks = gradient.shape[0]
    size_lo = 4
    size_hi = chunks // size_lo
    c = lax.axis_index("chan")
    hi, lo = c // size_lo, c % size_lo
    acc = gradient.reshape((2, size_hi // 2, size_lo) + gradient.shape[1:])
    for bit in (2, 1):
        mine = (hi // bit) % 2
        keep = lax.dynamic_index_in_dim(acc, mine, 0, keepdims=False)
        give = lax.dynamic_index_in_dim(acc, 1 - mine, 0, keepdims=False)
        pairs = [
            (h * size_lo + l, (h ^ bit) * size_lo + l) for h in range(size_hi) for l in range(size_lo)
        ]
        acc = keep + lax.ppermute(give, "chan", pairs)
    out = lax.dynamic_index_in_dim(acc, lo, 0, keepdims=False)
    for k in range(1, size_lo):
        piece = lax.dynamic_index_in_dim(acc, (lo + k) % size_lo, 0, keepdims=False)
        out = out + lax.ppermute(piece, "chan", _ring_pairs(size_hi, size_lo, k, True))
    return out


def shards(grid, tile_list, owner_map, offsets, positions, observed, weights):
    owners = lax.axis_size("bl")
    chan = lax.axis_size("chan")
    tile_dev = grid.shape[0]
    tile_width = grid.shape[1]
    block_count = tile_list.shape[1]
    capacity = 2 * block_count // owners
    slots_all = owners * capacity
    tile_ids = tile_list[0]
    slot_index = jnp.take(owner_map, tile_ids, axis=0)
    owner_index = slot_index // tile_dev
    local_slot = slot_index % tile_dev
    owner_onehot = (owner_index[:, None] == jnp.arange(owners, dtype=jnp.int32)[None, :]).astype(
        jnp.int32
    )
    earlier_count = jnp.cumsum(owner_onehot, axis=0) - owner_onehot
    place_rank = jnp.sum(owner_onehot * earlier_count, axis=1)
    send_slot = owner_index * capacity + place_rank
    coords = offsets[0].astype(jnp.float32)[..., None] + positions[0]
    vis = coords.shape[-1]
    label_row = jnp.broadcast_to(local_slot.astype(jnp.float32)[:, None, None], (block_count, 1, vis))
    payload = jnp.concatenate([observed[0], weights[0][:, None, :], coords, label_row], axis=1)
    match = send_slot[None, :] == jnp.arange(slots_all, dtype=jnp.int32)[:, None]
    source = jnp.sum(jnp.where(match, jnp.arange(block_count, dtype=jnp.int32)[None, :], 0), axis=1)
    source = jnp.where(jnp.any(match, axis=1), source, block_count)
    padded = jnp.concatenate([payload, jnp.zeros((1,) + payload.shape[1:], payload.dtype)], axis=0)
    outgoing = jnp.take(padded, source, axis=0)
    incoming = lax.all_to_all(outgoing, "bl", split_axis=0, concat_axis=0, tiled=True)
    labels = jnp.max(incoming[:, 5, :], axis=1).astype(jnp.int32)
    tiles_t = jnp.swapaxes(grid.astype(jnp.bfloat16), 1, 2)
    residual_all, gradient = _grid_call(labels, incoming, tiles_t, chan)
    share_rows = tile_width // chan
    grad_share = _chan_reduce(gradient)
    returned = lax.all_to_all(residual_all, "bl", split_axis=0, concat_axis=0, tiled=True)
    my_residual = jnp.take(returned, send_slot, axis=0)[None]
    share_start = lax.axis_index("chan") * share_rows
    own_rows = lax.dynamic_slice_in_dim(grid, share_start, share_rows, 1)
    new_grid = own_rows - step_length * (grad_share + ridge_weight * own_rows)
    return (new_grid, my_residual)


def solution(mesh):
    in_specs = (
        P("bl", None, None),
        P("chan", "bl"),
        P(),
        P("chan", "bl", None),
        P("chan", "bl", None, None),
        P("chan", "bl", None, None),
        P("chan", "bl", None),
    )
    out_specs = (P("bl", "chan", None), P("chan", "bl", None, None))
    return jax.shard_map(shards, mesh=mesh, in_specs=in_specs, out_specs=out_specs, check_vma=False)
```

```python
import functools

import jax
import jax.numpy as jnp
from jax import lax
from jax.experimental import pallas as pl
from jax.experimental.pallas import tpu as pltpu
from jax.sharding import PartitionSpec as P

kernel_beta = 18.4
half_support = 4.0
step_length = 1.0
ridge_weight = 0.5


def spheroid(offset):
    scaled = offset * (1.0 / half_support)
    inside = scaled * scaled < 1.0
    root_term = jnp.sqrt(jnp.maximum(1.0 - scaled * scaled, 0.0))
    return jnp.where(inside, jnp.exp(kernel_beta * (root_term - 1.0)), 0.0)


def _spheroid_scaled(scaled):
    inside = scaled * scaled < 1.0
    rest = 1.0 - scaled * scaled
    root_term = rest * lax.rsqrt(rest)
    return jnp.where(inside, jnp.exp(kernel_beta * (root_term - 1.0)), 0.0)


def _grid_kernel(labels_ref, data_ref, tiles_ref, res_ref, grad_ref):
    slots = data_ref.shape[0]
    chunks, _, rows, _ = grad_ref.shape
    width = tiles_ref.shape[2]
    vis = data_ref.shape[2]
    grad_ref[...] = jnp.zeros(grad_ref.shape, grad_ref.dtype)
    cells = lax.broadcasted_iota(jnp.int32, (width, vis), 0).astype(jnp.float32) * (1.0 / half_support)

    def body(s, carry):
        d = data_ref[s]
        tile = labels_ref[s]
        quarter = d[3:5, :] * (1.0 / half_support)
        ku_t = _spheroid_scaled(cells - quarter[0:1]).astype(jnp.bfloat16)
        kv_t = _spheroid_scaled(cells - quarter[1:2]).astype(jnp.bfloat16).astype(jnp.float32)
        proj_t = jnp.dot(tiles_ref[tile], ku_t, preferred_element_type=jnp.float32)
        model_re = jnp.sum(proj_t[:width] * kv_t, axis=0, keepdims=True)
        model_im = jnp.sum(proj_t[width:] * kv_t, axis=0, keepdims=True)
        weight = d[2:3, :]
        res_re = weight * (model_re - d[0:1, :])
        res_im = weight * (model_im - d[1:2, :])
        res_ref[s] = jnp.concatenate([res_re, res_im], axis=0)
        spread_t = jnp.concatenate([res_re * kv_t, res_im * kv_t], axis=0).astype(jnp.bfloat16)
        contrib = lax.dot_general(
            ku_t, spread_t, (((1,), (1,)), ((), ())), preferred_element_type=jnp.float32
        )
        grad_ref[:, pl.ds(tile, 1)] += contrib.reshape(chunks, 1, rows, 2 * width)
        return carry

    lax.fori_loop(0, slots, body, 0, unroll=32)


def _grid_call(labels, data, tiles_t, chunks):
    slots, _, vis = data.shape
    tile_count, wide, width = tiles_t.shape
    vmem = pltpu.MemorySpace.VMEM
    return pl.pallas_call(
        _grid_kernel,
        out_shape=(
            jax.ShapeDtypeStruct((slots, 2, vis), jnp.float32),
            jax.ShapeDtypeStruct((chunks, tile_count, width // chunks, wide), jnp.float32),
        ),
        in_specs=[
            pl.BlockSpec(memory_space=pltpu.MemorySpace.SMEM),
            pl.BlockSpec(memory_space=vmem),
            pl.BlockSpec(memory_space=vmem),
        ],
        out_specs=(pl.BlockSpec(memory_space=vmem), pl.BlockSpec(memory_space=vmem)),
    )(labels, data, tiles_t)


def _ring_pairs(size_hi, size_lo, shift, along_lo):
    pairs = []
    for hi in range(size_hi):
        for lo in range(size_lo):
            if along_lo:
                pairs.append((hi * size_lo + lo, hi * size_lo + (lo + shift) % size_lo))
            else:
                pairs.append((hi * size_lo + lo, ((hi + shift) % size_hi) * size_lo + lo))
    return pairs


def _chan_reduce(gradient):
    chunks = gradient.shape[0]
    size_lo = 4
    size_hi = chunks // size_lo
    c = lax.axis_index("chan")
    hi, lo = c // size_lo, c % size_lo
    parts = gradient.reshape((size_hi, size_lo) + gradient.shape[1:])
    acc = lax.dynamic_index_in_dim(parts, lo, 1, keepdims=False)
    for k in range(1, size_lo):
        piece = lax.dynamic_index_in_dim(parts, (lo + k) % size_lo, 1, keepdims=False)
        acc = acc + lax.ppermute(piece, "chan", _ring_pairs(size_hi, size_lo, k, True))
    for bit in (2, 1):
        halves = acc.reshape((2, acc.shape[0] // 2) + acc.shape[1:]) if bit == 2 else acc.reshape(
            (2, 1) + acc.shape[1:]
        )
        mine = (hi // bit) % 2
        keep = lax.dynamic_index_in_dim(halves, mine, 0, keepdims=False)
        give = lax.dynamic_index_in_dim(halves, 1 - mine, 0, keepdims=False)
        pairs = [
            (h * size_lo + l, (h ^ bit) * size_lo + l) for h in range(size_hi) for l in range(size_lo)
        ]
        acc = keep + lax.ppermute(give, "chan", pairs)
    return acc[0]


def _dispatch_kernel(tile_ref, owner_ref, off_ref, pos_ref, obs_ref, w_ref, out_ref, slot_ref, count_ref):
    blocks, _, vis = pos_ref.shape
    owners = count_ref.shape[0]
    capacity = out_ref.shape[0] // owners
    tile_dev = owner_ref.shape[0] // owners
    out_ref[...] = jnp.zeros(out_ref.shape, out_ref.dtype)

    def clear(o, carry):
        count_ref[o] = 0
        return carry

    lax.fori_loop(0, owners, clear, 0)

    def body(b, carry):
        slot = owner_ref[tile_ref[b]]
        owner = slot // tile_dev
        local = slot % tile_dev
        rank = jnp.minimum(count_ref[owner], capacity - 1)
        count_ref[owner] = rank + 1
        dest = owner * capacity + rank
        slot_ref[b] = dest
        pos = pos_ref[b]
        coord_u = off_ref[2 * b].astype(jnp.float32) + pos[0:1]
        coord_v = off_ref[2 * b + 1].astype(jnp.float32) + pos[1:2]
        label = jnp.full((1, vis), local.astype(jnp.float32), jnp.float32)
        out_ref[dest] = jnp.concatenate(
            [obs_ref[b], w_ref[pl.ds(b, 1), :], coord_u, coord_v, label], axis=0
        )
        return carry

    lax.fori_loop(0, blocks, body, 0)


def _dispatch_call(tile_ids, owner_map, offsets, positions, observed, weights, owners, capacity):
    blocks, _, vis = positions.shape
    smem = pltpu.MemorySpace.SMEM
    vmem = pltpu.MemorySpace.VMEM
    return pl.pallas_call(
        _dispatch_kernel,
        out_shape=(
            jax.ShapeDtypeStruct((owners * capacity, 6, vis), jnp.float32),
            jax.ShapeDtypeStruct((blocks,), jnp.int32),
        ),
        in_specs=[
            pl.BlockSpec(memory_space=smem),
            pl.BlockSpec(memory_space=smem),
            pl.BlockSpec(memory_space=smem),
            pl.BlockSpec(memory_space=vmem),
            pl.BlockSpec(memory_space=vmem),
            pl.BlockSpec(memory_space=vmem),
        ],
        out_specs=(pl.BlockSpec(memory_space=vmem), pl.BlockSpec(memory_space=smem)),
        scratch_shapes=[pltpu.SMEM((owners,), jnp.int32)],
    )(tile_ids, owner_map, offsets.reshape(-1), positions, observed, weights)


def shards(grid, tile_list, owner_map, offsets, positions, observed, weights):
    owners = lax.axis_size("bl")
    chan = lax.axis_size("chan")
    tile_dev = grid.shape[0]
    tile_width = grid.shape[1]
    block_count = tile_list.shape[1]
    capacity = 2 * block_count // owners
    slots_all = owners * capacity
    tile_ids = tile_list[0]
    outgoing, send_slot = _dispatch_call(
        tile_ids, owner_map, offsets[0], positions[0], observed[0], weights[0], owners, capacity
    )
    incoming = lax.all_to_all(outgoing, "bl", split_axis=0, concat_axis=0, tiled=True)
    labels = jnp.max(incoming[:, 5, :], axis=1).astype(jnp.int32)
    tiles_t = jnp.swapaxes(grid.astype(jnp.bfloat16), 1, 2)
    residual_all, gradient = _grid_call(labels, incoming, tiles_t, chan)
    share_rows = tile_width // chan
    grad_share = _chan_reduce(gradient)
    returned = lax.all_to_all(residual_all, "bl", split_axis=0, concat_axis=0, tiled=True)
    my_residual = jnp.take(returned, send_slot, axis=0)[None]
    share_start = lax.axis_index("chan") * share_rows
    own_rows = lax.dynamic_slice_in_dim(grid, share_start, share_rows, 1)
    new_grid = own_rows - step_length * (grad_share + ridge_weight * own_rows)
    return (new_grid, my_residual)


def solution(mesh):
    in_specs = (
        P("bl", None, None),
        P("chan", "bl"),
        P(),
        P("chan", "bl", None),
        P("chan", "bl", None, None),
        P("chan", "bl", None, None),
        P("chan", "bl", None),
    )
    out_specs = (P("bl", "chan", None), P("chan", "bl", None, None))
    return jax.shard_map(shards, mesh=mesh, in_specs=in_specs, out_specs=out_specs, check_vma=False)
```

```python
import functools

import jax
import jax.numpy as jnp
from jax import lax
from jax.experimental import pallas as pl
from jax.experimental.pallas import tpu as pltpu
from jax.sharding import PartitionSpec as P

kernel_beta = 18.4
half_support = 4.0
step_length = 1.0
ridge_weight = 0.5


def spheroid(offset):
    scaled = offset * (1.0 / half_support)
    inside = scaled * scaled < 1.0
    root_term = jnp.sqrt(jnp.maximum(1.0 - scaled * scaled, 0.0))
    return jnp.where(inside, jnp.exp(kernel_beta * (root_term - 1.0)), 0.0)


def _spheroid_scaled(scaled):
    inside = scaled * scaled < 1.0
    rest = 1.0 - scaled * scaled
    root_term = rest * lax.rsqrt(rest)
    return jnp.where(inside, jnp.exp(kernel_beta * (root_term - 1.0)), 0.0)


def _grid_kernel(labels_ref, data_ref, tiles_ref, res_ref, grad_ref):
    slots = data_ref.shape[0]
    chunks, _, rows, _ = grad_ref.shape
    width = tiles_ref.shape[2]
    vis = data_ref.shape[2]
    grad_ref[...] = jnp.zeros(grad_ref.shape, grad_ref.dtype)
    cells = lax.broadcasted_iota(jnp.int32, (width, vis), 0).astype(jnp.float32) * (1.0 / half_support)

    def body(s, carry):
        d = data_ref[s]
        tile = labels_ref[s]
        quarter = d[3:5, :] * (1.0 / half_support)
        ku_t = _spheroid_scaled(cells - quarter[0:1]).astype(jnp.bfloat16)
        kv_t = _spheroid_scaled(cells - quarter[1:2]).astype(jnp.bfloat16).astype(jnp.float32)
        proj_t = jnp.dot(tiles_ref[tile], ku_t, preferred_element_type=jnp.float32)
        model_re = jnp.sum(proj_t[:width] * kv_t, axis=0, keepdims=True)
        model_im = jnp.sum(proj_t[width:] * kv_t, axis=0, keepdims=True)
        weight = d[2:3, :]
        res_re = weight * (model_re - d[0:1, :])
        res_im = weight * (model_im - d[1:2, :])
        res_ref[s] = jnp.concatenate([res_re, res_im], axis=0)
        spread_t = jnp.concatenate([res_re * kv_t, res_im * kv_t], axis=0).astype(jnp.bfloat16)
        contrib = lax.dot_general(
            ku_t, spread_t, (((1,), (1,)), ((), ())), preferred_element_type=jnp.float32
        )
        grad_ref[:, pl.ds(tile, 1)] += contrib.reshape(chunks, 1, rows, 2 * width)
        return carry

    lax.fori_loop(0, slots, body, 0, unroll=32)


def _grid_call(labels, data, tiles_t, chunks):
    slots, _, vis = data.shape
    tile_count, wide, width = tiles_t.shape
    vmem = pltpu.MemorySpace.VMEM
    return pl.pallas_call(
        _grid_kernel,
        out_shape=(
            jax.ShapeDtypeStruct((slots, 2, vis), jnp.float32),
            jax.ShapeDtypeStruct((chunks, tile_count, width // chunks, wide), jnp.float32),
        ),
        in_specs=[
            pl.BlockSpec(memory_space=pltpu.MemorySpace.SMEM),
            pl.BlockSpec(memory_space=vmem),
            pl.BlockSpec(memory_space=vmem),
        ],
        out_specs=(pl.BlockSpec(memory_space=vmem), pl.BlockSpec(memory_space=vmem)),
    )(labels, data, tiles_t)


def _ring_pairs(size_hi, size_lo, shift, along_lo):
    pairs = []
    for hi in range(size_hi):
        for lo in range(size_lo):
            if along_lo:
                pairs.append((hi * size_lo + lo, hi * size_lo + (lo + shift) % size_lo))
            else:
                pairs.append((hi * size_lo + lo, ((hi + shift) % size_hi) * size_lo + lo))
    return pairs


def _chan_reduce(gradient):
    chunks = gradient.shape[0]
    size_lo = 4
    size_hi = chunks // size_lo
    c = lax.axis_index("chan")
    hi, lo = c // size_lo, c % size_lo
    parts = gradient.reshape((size_hi, size_lo) + gradient.shape[1:])
    acc = lax.dynamic_index_in_dim(parts, lo, 1, keepdims=False)
    for k in range(1, size_lo):
        piece = lax.dynamic_index_in_dim(parts, (lo + k) % size_lo, 1, keepdims=False)
        acc = acc + lax.ppermute(piece, "chan", _ring_pairs(size_hi, size_lo, k, True))
    for bit in (2, 1):
        halves = acc.reshape((2, acc.shape[0] // 2) + acc.shape[1:]) if bit == 2 else acc.reshape(
            (2, 1) + acc.shape[1:]
        )
        mine = (hi // bit) % 2
        keep = lax.dynamic_index_in_dim(halves, mine, 0, keepdims=False)
        give = lax.dynamic_index_in_dim(halves, 1 - mine, 0, keepdims=False)
        pairs = [
            (h * size_lo + l, (h ^ bit) * size_lo + l) for h in range(size_hi) for l in range(size_lo)
        ]
        acc = keep + lax.ppermute(give, "chan", pairs)
    return acc[0]


def _dispatch_kernel(tile_ref, owner_ref, off_ref, pos_ref, obs_ref, w_ref, out_ref, slot_ref, count_ref):
    blocks, _, vis = pos_ref.shape
    owners = count_ref.shape[0]
    capacity = out_ref.shape[0] // owners
    tile_dev = owner_ref.shape[0] // owners
    out_ref[...] = jnp.zeros(out_ref.shape, out_ref.dtype)

    def clear(o, carry):
        count_ref[o] = 0
        return carry

    lax.fori_loop(0, owners, clear, 0)

    def body(b, carry):
        slot = owner_ref[tile_ref[b]]
        owner = slot // tile_dev
        local = slot % tile_dev
        rank = jnp.minimum(count_ref[owner], capacity - 1)
        count_ref[owner] = rank + 1
        dest = owner * capacity + rank
        slot_ref[b] = dest
        pos = pos_ref[b]
        coord_u = off_ref[b, 0].astype(jnp.float32) + pos[0:1]
        coord_v = off_ref[b, 1].astype(jnp.float32) + pos[1:2]
        label = jnp.full((1, vis), local.astype(jnp.float32), jnp.float32)
        out_ref[dest] = jnp.concatenate(
            [obs_ref[b], w_ref[pl.ds(b, 1), :], coord_u, coord_v, label], axis=0
        )
        return carry

    lax.fori_loop(0, blocks, body, 0, unroll=8)


def _dispatch_call(tile_ids, owner_map, offsets, positions, observed, weights, owners, capacity):
    blocks, _, vis = positions.shape
    smem = pltpu.MemorySpace.SMEM
    vmem = pltpu.MemorySpace.VMEM
    return pl.pallas_call(
        _dispatch_kernel,
        out_shape=(
            jax.ShapeDtypeStruct((owners * capacity, 6, vis), jnp.float32),
            jax.ShapeDtypeStruct((blocks,), jnp.int32),
        ),
        in_specs=[
            pl.BlockSpec(memory_space=smem),
            pl.BlockSpec(memory_space=smem),
            pl.BlockSpec(memory_space=smem),
            pl.BlockSpec(memory_space=vmem),
            pl.BlockSpec(memory_space=vmem),
            pl.BlockSpec(memory_space=vmem),
        ],
        out_specs=(pl.BlockSpec(memory_space=vmem), pl.BlockSpec(memory_space=smem)),
        scratch_shapes=[pltpu.SMEM((owners,), jnp.int32)],
    )(tile_ids, owner_map, offsets, positions, observed, weights)


def shards(grid, tile_list, owner_map, offsets, positions, observed, weights):
    owners = lax.axis_size("bl")
    chan = lax.axis_size("chan")
    tile_dev = grid.shape[0]
    tile_width = grid.shape[1]
    block_count = tile_list.shape[1]
    capacity = 2 * block_count // owners
    slots_all = owners * capacity
    tile_ids = tile_list[0]
    outgoing, send_slot = _dispatch_call(
        tile_ids, owner_map, offsets[0], positions[0], observed[0], weights[0], owners, capacity
    )
    incoming = lax.all_to_all(outgoing, "bl", split_axis=0, concat_axis=0, tiled=True)
    labels = jnp.max(incoming[:, 5, :], axis=1).astype(jnp.int32)
    tiles_t = jnp.swapaxes(grid.astype(jnp.bfloat16), 1, 2)
    residual_all, gradient = _grid_call(labels, incoming, tiles_t, chan)
    share_rows = tile_width // chan
    grad_share = _chan_reduce(gradient)
    returned = lax.all_to_all(residual_all, "bl", split_axis=0, concat_axis=0, tiled=True)
    my_residual = jnp.take(returned, send_slot, axis=0)[None]
    share_start = lax.axis_index("chan") * share_rows
    own_rows = lax.dynamic_slice_in_dim(grid, share_start, share_rows, 1)
    new_grid = own_rows - step_length * (grad_share + ridge_weight * own_rows)
    return (new_grid, my_residual)


def solution(mesh):
    in_specs = (
        P("bl", None, None),
        P("chan", "bl"),
        P(),
        P("chan", "bl", None),
        P("chan", "bl", None, None),
        P("chan", "bl", None, None),
        P("chan", "bl", None),
    )
    out_specs = (P("bl", "chan", None), P("chan", "bl", None, None))
    return jax.shard_map(shards, mesh=mesh, in_specs=in_specs, out_specs=out_specs, check_vma=False)
```

```python
import functools

import jax
import jax.numpy as jnp
from jax import lax
from jax.experimental import pallas as pl
from jax.experimental.pallas import tpu as pltpu
from jax.sharding import PartitionSpec as P

kernel_beta = 18.4
half_support = 4.0
step_length = 1.0
ridge_weight = 0.5


def spheroid(offset):
    scaled = offset * (1.0 / half_support)
    inside = scaled * scaled < 1.0
    root_term = jnp.sqrt(jnp.maximum(1.0 - scaled * scaled, 0.0))
    return jnp.where(inside, jnp.exp(kernel_beta * (root_term - 1.0)), 0.0)


def _spheroid_scaled(scaled):
    inside = scaled * scaled < 1.0
    rest = 1.0 - scaled * scaled
    root_term = rest * lax.rsqrt(rest)
    return jnp.where(inside, jnp.exp(kernel_beta * (root_term - 1.0)), 0.0)


def _grid_kernel(labels_ref, place_ref, data_ref, tiles_ref, res_ref, grad_ref):
    slots = data_ref.shape[0]
    ring, size_hi, _, rows, _ = grad_ref.shape
    place = place_ref[0]
    width = tiles_ref.shape[2]
    vis = data_ref.shape[2]
    grad_ref[...] = jnp.zeros(grad_ref.shape, grad_ref.dtype)
    cells = lax.broadcasted_iota(jnp.int32, (width, vis), 0).astype(jnp.float32) * (1.0 / half_support)

    def body(s, carry):
        d = data_ref[s]
        tile = labels_ref[s].astype(jnp.int32)
        quarter = d[3:5, :] * (1.0 / half_support)
        ku_t = _spheroid_scaled(cells - quarter[0:1]).astype(jnp.bfloat16)
        kv_t = _spheroid_scaled(cells - quarter[1:2]).astype(jnp.bfloat16).astype(jnp.float32)
        proj_t = jnp.dot(tiles_ref[tile], ku_t, preferred_element_type=jnp.float32)
        model_re = jnp.sum(proj_t[:width] * kv_t, axis=0, keepdims=True)
        model_im = jnp.sum(proj_t[width:] * kv_t, axis=0, keepdims=True)
        weight = d[2:3, :]
        res_re = weight * (model_re - d[0:1, :])
        res_im = weight * (model_im - d[1:2, :])
        res_ref[s] = jnp.concatenate([res_re, res_im], axis=0)
        spread_t = jnp.concatenate([res_re * kv_t, res_im * kv_t], axis=0).astype(jnp.bfloat16)
        contrib = lax.dot_general(
            ku_t, spread_t, (((1,), (1,)), ((), ())), preferred_element_type=jnp.float32
        )
        pieces = contrib.reshape(size_hi, ring, 1, rows, 2 * width)
        for x in range(ring):
            shift = (x - place + ring) % ring
            grad_ref[pl.ds(shift, 1), :, pl.ds(tile, 1)] += pieces[:, x][None]
        return carry

    lax.fori_loop(0, slots, body, 0, unroll=32)


def _grid_call(labels, place, data, tiles_t, chunks, ring):
    slots, _, vis = data.shape
    tile_count, wide, width = tiles_t.shape
    vmem = pltpu.MemorySpace.VMEM
    return pl.pallas_call(
        _grid_kernel,
        out_shape=(
            jax.ShapeDtypeStruct((slots, 2, vis), jnp.float32),
            jax.ShapeDtypeStruct(
                (ring, chunks // ring, tile_count, width // chunks, wide), jnp.float32
            ),
        ),
        in_specs=[
            pl.BlockSpec(memory_space=pltpu.MemorySpace.SMEM),
            pl.BlockSpec(memory_space=pltpu.MemorySpace.SMEM),
            pl.BlockSpec(memory_space=vmem),
            pl.BlockSpec(memory_space=vmem),
        ],
        out_specs=(pl.BlockSpec(memory_space=vmem), pl.BlockSpec(memory_space=vmem)),
    )(labels, place, data, tiles_t)


def _ring_pairs(size_hi, size_lo, shift, along_lo):
    pairs = []
    for hi in range(size_hi):
        for lo in range(size_lo):
            if along_lo:
                pairs.append((hi * size_lo + lo, hi * size_lo + (lo + shift) % size_lo))
            else:
                pairs.append((hi * size_lo + lo, ((hi + shift) % size_hi) * size_lo + lo))
    return pairs


def _chan_reduce(gradient):
    size_lo, size_hi = gradient.shape[0], gradient.shape[1]
    c = lax.axis_index("chan")
    hi, lo = c // size_lo, c % size_lo
    acc = gradient[0]
    for k in range(1, size_lo):
        acc = acc + lax.ppermute(gradient[k], "chan", _ring_pairs(size_hi, size_lo, k, True))
    for bit in (2, 1):
        halves = acc.reshape((2, acc.shape[0] // 2) + acc.shape[1:]) if bit == 2 else acc.reshape(
            (2, 1) + acc.shape[1:]
        )
        mine = (hi // bit) % 2
        keep = lax.dynamic_index_in_dim(halves, mine, 0, keepdims=False)
        give = lax.dynamic_index_in_dim(halves, 1 - mine, 0, keepdims=False)
        pairs = [
            (h * size_lo + l, (h ^ bit) * size_lo + l) for h in range(size_hi) for l in range(size_lo)
        ]
        acc = keep + lax.ppermute(give, "chan", pairs)
    return acc[0]


def _dispatch_kernel(tile_ref, owner_ref, off_ref, pos_ref, obs_ref, w_ref, out_ref, slot_ref, count_ref):
    blocks, _, vis = pos_ref.shape
    owners = count_ref.shape[0]
    capacity = out_ref.shape[0] // owners
    tile_dev = owner_ref.shape[0] // owners
    out_ref[...] = jnp.zeros(out_ref.shape, out_ref.dtype)

    def clear(o, carry):
        count_ref[o] = 0
        return carry

    lax.fori_loop(0, owners, clear, 0)

    def body(b, carry):
        slot = owner_ref[tile_ref[b]]
        owner = slot // tile_dev
        local = slot % tile_dev
        rank = jnp.minimum(count_ref[owner], capacity - 1)
        count_ref[owner] = rank + 1
        dest = owner * capacity + rank
        slot_ref[b] = dest
        pos = pos_ref[b]
        coord_u = off_ref[2 * b].astype(jnp.float32) + pos[0:1]
        coord_v = off_ref[2 * b + 1].astype(jnp.float32) + pos[1:2]
        label = jnp.full((1, vis), local.astype(jnp.float32), jnp.float32)
        out_ref[dest] = jnp.concatenate(
            [obs_ref[b], w_ref[pl.ds(b, 1), :], coord_u, coord_v, label], axis=0
        )
        return carry

    lax.fori_loop(0, blocks, body, 0)


def _dispatch_call(tile_ids, owner_map, offsets, positions, observed, weights, owners, capacity):
    blocks, _, vis = positions.shape
    smem = pltpu.MemorySpace.SMEM
    vmem = pltpu.MemorySpace.VMEM
    return pl.pallas_call(
        _dispatch_kernel,
        out_shape=(
            jax.ShapeDtypeStruct((owners * capacity, 6, vis), jnp.float32),
            jax.ShapeDtypeStruct((blocks,), jnp.int32),
        ),
        in_specs=[
            pl.BlockSpec(memory_space=smem),
            pl.BlockSpec(memory_space=smem),
            pl.BlockSpec(memory_space=smem),
            pl.BlockSpec(memory_space=vmem),
            pl.BlockSpec(memory_space=vmem),
            pl.BlockSpec(memory_space=vmem),
        ],
        out_specs=(pl.BlockSpec(memory_space=vmem), pl.BlockSpec(memory_space=smem)),
        scratch_shapes=[pltpu.SMEM((owners,), jnp.int32)],
    )(tile_ids, owner_map, offsets.reshape(-1), positions, observed, weights)


def shards(grid, tile_list, owner_map, offsets, positions, observed, weights):
    owners = lax.axis_size("bl")
    chan = lax.axis_size("chan")
    tile_dev = grid.shape[0]
    tile_width = grid.shape[1]
    block_count = tile_list.shape[1]
    capacity = 2 * block_count // owners
    slots_all = owners * capacity
    tile_ids = tile_list[0]
    outgoing, send_slot = _dispatch_call(
        tile_ids, owner_map, offsets[0], positions[0], observed[0], weights[0], owners, capacity
    )
    incoming = lax.all_to_all(outgoing, "bl", split_axis=0, concat_axis=0, tiled=True)
    labels = jnp.max(incoming[:, 5, :], axis=1)
    ring = 4
    place = (lax.axis_index("chan") % ring).astype(jnp.int32).reshape(1)
    tiles_t = jnp.swapaxes(grid.astype(jnp.bfloat16), 1, 2)
    residual_all, gradient = _grid_call(labels, place, incoming, tiles_t, chan, ring)
    share_rows = tile_width // chan
    grad_share = _chan_reduce(gradient)
    returned = lax.all_to_all(residual_all, "bl", split_axis=0, concat_axis=0, tiled=True)
    my_residual = jnp.take(returned, send_slot, axis=0)[None]
    share_start = lax.axis_index("chan") * share_rows
    own_rows = lax.dynamic_slice_in_dim(grid, share_start, share_rows, 1)
    new_grid = own_rows - step_length * (grad_share + ridge_weight * own_rows)
    return (new_grid, my_residual)


def solution(mesh):
    in_specs = (
        P("bl", None, None),
        P("chan", "bl"),
        P(),
        P("chan", "bl", None),
        P("chan", "bl", None, None),
        P("chan", "bl", None, None),
        P("chan", "bl", None),
    )
    out_specs = (P("bl", "chan", None), P("chan", "bl", None, None))
    return jax.shard_map(shards, mesh=mesh, in_specs=in_specs, out_specs=out_specs, check_vma=False)
```

```python
import functools

import jax
import jax.numpy as jnp
from jax import lax
from jax.experimental import pallas as pl
from jax.experimental.pallas import tpu as pltpu
from jax.sharding import PartitionSpec as P

kernel_beta = 18.4
half_support = 4.0
step_length = 1.0
ridge_weight = 0.5


def spheroid(offset):
    scaled = offset * (1.0 / half_support)
    inside = scaled * scaled < 1.0
    root_term = jnp.sqrt(jnp.maximum(1.0 - scaled * scaled, 0.0))
    return jnp.where(inside, jnp.exp(kernel_beta * (root_term - 1.0)), 0.0)


def _spheroid_scaled(scaled):
    inside = scaled * scaled < 1.0
    rest = 1.0 - scaled * scaled
    root_term = rest * lax.rsqrt(rest)
    return jnp.where(inside, jnp.exp(kernel_beta * (root_term - 1.0)), 0.0)


def _grid_kernel(labels_ref, data_ref, tiles_ref, res_ref, grad_ref):
    slots = data_ref.shape[0]
    chunks, _, rows, _ = grad_ref.shape
    width = tiles_ref.shape[2]
    vis = data_ref.shape[2]
    grad_ref[...] = jnp.zeros(grad_ref.shape, grad_ref.dtype)
    cells = lax.broadcasted_iota(jnp.int32, (width, vis), 0).astype(jnp.float32) * (1.0 / half_support)

    def body(s, carry):
        d = data_ref[s]
        tile = labels_ref[s]
        quarter = d[3:5, :] * (1.0 / half_support)
        ku_t = _spheroid_scaled(cells - quarter[0:1]).astype(jnp.bfloat16)
        kv_t = _spheroid_scaled(cells - quarter[1:2]).astype(jnp.bfloat16).astype(jnp.float32)
        proj_t = jnp.dot(tiles_ref[tile], ku_t, preferred_element_type=jnp.float32)
        model_re = jnp.sum(proj_t[:width] * kv_t, axis=0, keepdims=True)
        model_im = jnp.sum(proj_t[width:] * kv_t, axis=0, keepdims=True)
        weight = d[2:3, :]
        res_re = weight * (model_re - d[0:1, :])
        res_im = weight * (model_im - d[1:2, :])
        res_ref[s] = jnp.concatenate([res_re, res_im], axis=0)
        spread_t = jnp.concatenate([res_re * kv_t, res_im * kv_t], axis=0).astype(jnp.bfloat16)
        contrib = lax.dot_general(
            ku_t, spread_t, (((1,), (1,)), ((), ())), preferred_element_type=jnp.float32
        )
        grad_ref[:, pl.ds(tile, 1)] += contrib.reshape(chunks, 1, rows, 2 * width)
        return carry

    lax.fori_loop(0, slots, body, 0, unroll=64)


def _grid_call(labels, data, tiles_t, chunks):
    slots, _, vis = data.shape
    tile_count, wide, width = tiles_t.shape
    vmem = pltpu.MemorySpace.VMEM
    return pl.pallas_call(
        _grid_kernel,
        out_shape=(
            jax.ShapeDtypeStruct((slots, 2, vis), jnp.float32),
            jax.ShapeDtypeStruct((chunks, tile_count, width // chunks, wide), jnp.float32),
        ),
        in_specs=[
            pl.BlockSpec(memory_space=pltpu.MemorySpace.SMEM),
            pl.BlockSpec(memory_space=vmem),
            pl.BlockSpec(memory_space=vmem),
        ],
        out_specs=(pl.BlockSpec(memory_space=vmem), pl.BlockSpec(memory_space=vmem)),
    )(labels, data, tiles_t)


def _ring_pairs(size_hi, size_lo, shift, along_lo):
    pairs = []
    for hi in range(size_hi):
        for lo in range(size_lo):
            if along_lo:
                pairs.append((hi * size_lo + lo, hi * size_lo + (lo + shift) % size_lo))
            else:
                pairs.append((hi * size_lo + lo, ((hi + shift) % size_hi) * size_lo + lo))
    return pairs


def _chan_reduce(gradient):
    chunks = gradient.shape[0]
    size_lo = 4
    size_hi = chunks // size_lo
    c = lax.axis_index("chan")
    hi, lo = c // size_lo, c % size_lo
    parts = gradient.reshape((size_hi, size_lo) + gradient.shape[1:])
    acc = lax.dynamic_index_in_dim(parts, lo, 1, keepdims=False)
    for k in range(1, size_lo):
        piece = lax.dynamic_index_in_dim(parts, (lo + k) % size_lo, 1, keepdims=False)
        acc = acc + lax.ppermute(piece, "chan", _ring_pairs(size_hi, size_lo, k, True))
    for bit in (2, 1):
        halves = acc.reshape((2, acc.shape[0] // 2) + acc.shape[1:]) if bit == 2 else acc.reshape(
            (2, 1) + acc.shape[1:]
        )
        mine = (hi // bit) % 2
        keep = lax.dynamic_index_in_dim(halves, mine, 0, keepdims=False)
        give = lax.dynamic_index_in_dim(halves, 1 - mine, 0, keepdims=False)
        pairs = [
            (h * size_lo + l, (h ^ bit) * size_lo + l) for h in range(size_hi) for l in range(size_lo)
        ]
        acc = keep + lax.ppermute(give, "chan", pairs)
    return acc[0]


def _dispatch_kernel(tile_ref, owner_ref, off_ref, pos_ref, obs_ref, w_ref, out_ref, slot_ref, count_ref):
    blocks, _, vis = pos_ref.shape
    owners = count_ref.shape[0]
    capacity = out_ref.shape[0] // owners
    tile_dev = owner_ref.shape[0] // owners
    out_ref[...] = jnp.zeros(out_ref.shape, out_ref.dtype)

    def clear(o, carry):
        count_ref[o] = 0
        return carry

    lax.fori_loop(0, owners, clear, 0)

    def body(b, carry):
        slot = owner_ref[tile_ref[b]]
        owner = slot // tile_dev
        local = slot % tile_dev
        rank = jnp.minimum(count_ref[owner], capacity - 1)
        count_ref[owner] = rank + 1
        dest = owner * capacity + rank
        slot_ref[b] = dest
        pos = pos_ref[b]
        coord_u = off_ref[2 * b].astype(jnp.float32) + pos[0:1]
        coord_v = off_ref[2 * b + 1].astype(jnp.float32) + pos[1:2]
        label = jnp.full((1, vis), local.astype(jnp.float32), jnp.float32)
        out_ref[dest] = jnp.concatenate(
            [obs_ref[b], w_ref[pl.ds(b, 1), :], coord_u, coord_v, label], axis=0
        )
        return carry

    lax.fori_loop(0, blocks, body, 0)


def _dispatch_call(tile_ids, owner_map, offsets, positions, observed, weights, owners, capacity):
    blocks, _, vis = positions.shape
    smem = pltpu.MemorySpace.SMEM
    vmem = pltpu.MemorySpace.VMEM
    return pl.pallas_call(
        _dispatch_kernel,
        out_shape=(
            jax.ShapeDtypeStruct((owners * capacity, 6, vis), jnp.float32),
            jax.ShapeDtypeStruct((blocks,), jnp.int32),
        ),
        in_specs=[
            pl.BlockSpec(memory_space=smem),
            pl.BlockSpec(memory_space=smem),
            pl.BlockSpec(memory_space=smem),
            pl.BlockSpec(memory_space=vmem),
            pl.BlockSpec(memory_space=vmem),
            pl.BlockSpec(memory_space=vmem),
        ],
        out_specs=(pl.BlockSpec(memory_space=vmem), pl.BlockSpec(memory_space=smem)),
        scratch_shapes=[pltpu.SMEM((owners,), jnp.int32)],
    )(tile_ids, owner_map, offsets.reshape(-1), positions, observed, weights)


def shards(grid, tile_list, owner_map, offsets, positions, observed, weights):
    owners = lax.axis_size("bl")
    chan = lax.axis_size("chan")
    tile_dev = grid.shape[0]
    tile_width = grid.shape[1]
    block_count = tile_list.shape[1]
    capacity = 2 * block_count // owners
    slots_all = owners * capacity
    tile_ids = tile_list[0]
    outgoing, send_slot = _dispatch_call(
        tile_ids, owner_map, offsets[0], positions[0], observed[0], weights[0], owners, capacity
    )
    incoming = lax.all_to_all(outgoing, "bl", split_axis=0, concat_axis=0, tiled=True)
    labels = jnp.max(incoming[:, 5, :], axis=1).astype(jnp.int32)
    tiles_t = jnp.swapaxes(grid.astype(jnp.bfloat16), 1, 2)
    residual_all, gradient = _grid_call(labels, incoming, tiles_t, chan)
    share_rows = tile_width // chan
    grad_share = _chan_reduce(gradient)
    returned = lax.all_to_all(residual_all, "bl", split_axis=0, concat_axis=0, tiled=True)
    my_residual = jnp.take(returned, send_slot, axis=0)[None]
    share_start = lax.axis_index("chan") * share_rows
    own_rows = lax.dynamic_slice_in_dim(grid, share_start, share_rows, 1)
    new_grid = own_rows - step_length * (grad_share + ridge_weight * own_rows)
    return (new_grid, my_residual)


def solution(mesh):
    in_specs = (
        P("bl", None, None),
        P("chan", "bl"),
        P(),
        P("chan", "bl", None),
        P("chan", "bl", None, None),
        P("chan", "bl", None, None),
        P("chan", "bl", None),
    )
    out_specs = (P("bl", "chan", None), P("chan", "bl", None, None))
    return jax.shard_map(shards, mesh=mesh, in_specs=in_specs, out_specs=out_specs, check_vma=False)
```
